128 devices in a mesh: gx: 8 (over y, core), gy: 16 (over x, z).
Axes of the slice: x: 4, y: 4, z: 4, core: 2. Of those that a mesh axis runs over, the one named last changes fastest.
Arguments:
- scalars: float32 [4, 512, 512, 128], P(None, 'gx', 'gy'), may hold values from -6 to 6
- velocity: float32 [3, 512, 512, 128], P(None, 'gx', 'gy'), may hold values from -12 to 12
- diffusivity: float32 [512, 512, 128], P('gx', 'gy'), may hold values from 0.05 to 0.6
- diff_scale: float32 [4], replicated, may hold values from 0.3 to 1
- basis_old: bfloat16 [48, 256, 16384], P(None, 'gx', 'gy'), may hold values from -5 to 5
- sing_values: float32 [48], replicated, may hold values from 0.5 to 2
- stored: bfloat16 [16, 256, 16384], P(None, 'gx', 'gy'), may hold values from -9 to 9
Outputs:
- scalars_out: float32 [4, 512, 512, 128], P(None, 'gx', 'gy')
- basis_new: float32 [65, 256, 16384], P(None, 'gx', 'gy')
- factor: float32 [65, 65], replicated
The draws below stay inside these ranges and needn't reach their ends.
All inputs are finite; a program needn't handle non-finite values.
Results may differ from the reference program's by a relative error of at most 0.0003.
Values sent between devices are 32-bit elements; how exact they have to be, the bound alone decides.
No kernel may reach another device: no remote copies, remote signals or barrier semaphores. Data moves between devices by JAX's collectives and lax.ppermute only.
A program may use at most 192 MiB of HBM per device.

```python
import math
import jax
import jax.numpy as jnp
from jax import lax

SCALARS = 4
RANK = 48
SNAPS = 16
NZ = 128
NX = 512
NY = 512
HX = 256
HY = 256
HZ = 64


def basis_common(key):
    values = jax.random.normal(jax.random.fold_in(key, 11), (RANK, HX, HY * HZ), jnp.float32)
    return jnp.clip(values, -5.0, 5.0)


def draw_basis_old(key, part):
    return basis_common(key).astype(jnp.bfloat16)


def draw_stored(key, part):
    base = basis_common(key)
    noise = jnp.clip(jax.random.normal(jax.random.fold_in(key, 23), (SNAPS, HX, HY * HZ), jnp.float32), -5.0, 5.0)
    mixed = 0.7 * base[:SNAPS] + 0.5 * base[SNAPS:2 * SNAPS] + 0.6 * noise
    return mixed.astype(jnp.bfloat16)


def shard_levels(key, shape, shards, least, high):
    def one(axis_at, shards_of):
        heights = jax.random.uniform(jax.random.fold_in(jax.random.fold_in(key, 6), axis_at), (shards_of,), jnp.float32, least / len(shards), high / len(shards))
        return jnp.repeat(jnp.exp(heights), shape[axis_at] // shards_of).reshape((-1,) + (1,) * (len(shape) - axis_at - 1))

    factor_of = one(*shards[0])
    for cut in shards[1:]:
        factor_of = factor_of * one(*cut)
    return factor_of


def gaussian(rng, shape, width, reach, cuts=(), kind=jnp.bfloat16):
    entries = width * jax.random.normal(rng, shape, jnp.float32)
    if cuts:
        entries = entries * shard_levels(rng, shape, cuts, -0.22, 0.18)
    return jnp.clip(entries, -reach, reach).astype(kind)


def setup_inputs(seed: int = 0) -> dict:
    keys = jax.random.split(jax.random.key(seed), 8)
    scalars = gaussian(keys[0], (SCALARS, NX, NY, NZ), 1.0, 6.0, ((1, 8), (2, 16)), jnp.float32)
    velocity = gaussian(keys[1], (3, NX, NY, NZ), 2.0, 12.0, ((1, 8), (2, 16)), jnp.float32)
    diffusivity = jnp.clip(0.05 + 0.55 * jax.random.uniform(keys[2], (NX, NY, NZ), jnp.float32) ** shard_levels(keys[2], (NX, NY, NZ), ((0, 8), (1, 16)), -0.2, 0.2), 0.05, 0.6)
    diff_scale = jnp.clip(jnp.exp(jax.random.uniform(keys[3], (SCALARS,), jnp.float32, math.log(0.3), math.log(1.0))), 0.3, 1.0)
    basis_old = draw_basis_old(jax.random.fold_in(keys[7], 71), 0)
    sing_values = jnp.clip(jnp.exp(jax.random.uniform(keys[5], (RANK,), jnp.float32, math.log(0.5), math.log(2.0))), 0.5, 2.0)
    stored = draw_stored(jax.random.fold_in(keys[7], 71), 0)
    return dict(scalars=scalars, velocity=velocity, diffusivity=diffusivity, diff_scale=diff_scale, basis_old=basis_old, sing_values=sing_values, stored=stored)


time_step = 0.25

def tendency(concen, coeffs, diff_scale):
    velocity = coeffs[:3]
    kappa = coeffs[3]
    center = concen[:, 2:-2, 2:-2, :]
    flux_first = velocity[0][None] * concen
    slope = (8.0 * (flux_first[:, 3:-1, 2:-2] - flux_first[:, 1:-3, 2:-2]) - (flux_first[:, 4:, 2:-2] - flux_first[:, :-4, 2:-2])) / 12.0
    flux_second = velocity[1][None] * concen
    slope = slope + (8.0 * (flux_second[:, 2:-2, 3:-1] - flux_second[:, 2:-2, 1:-3]) - (flux_second[:, 2:-2, 4:] - flux_second[:, 2:-2, :-4])) / 12.0
    flux_third = jnp.pad(velocity[2][2:-2, 2:-2][None] * center, ((0, 0), (0, 0), (0, 0), (2, 2)))
    slope = slope + (8.0 * (flux_third[..., 3:-1] - flux_third[..., 1:-3]) - (flux_third[..., 4:] - flux_third[..., :-4])) / 12.0
    kappa_mid = kappa[2:-2, 2:-2][None]
    spread = (kappa_mid + kappa[3:-1, 2:-2][None]) * 0.5 * (concen[:, 3:-1, 2:-2] - center) - (kappa_mid + kappa[1:-3, 2:-2][None]) * 0.5 * (center - concen[:, 1:-3, 2:-2])
    spread = spread + (kappa_mid + kappa[2:-2, 3:-1][None]) * 0.5 * (concen[:, 2:-2, 3:-1] - center) - (kappa_mid + kappa[2:-2, 1:-3][None]) * 0.5 * (center - concen[:, 2:-2, 1:-3])
    kappa_pad = jnp.pad(kappa_mid, ((0, 0), (0, 0), (0, 0), (1, 1)))
    center_pad = jnp.pad(center, ((0, 0), (0, 0), (0, 0), (1, 1)))
    spread = spread + (kappa_mid + kappa_pad[..., 2:]) * 0.5 * (center_pad[..., 2:] - center) - (kappa_mid + kappa_pad[..., :-2]) * 0.5 * (center - center_pad[..., :-2])
    return center + time_step * (diff_scale[:, None, None, None] * spread - slope)

def reference(scalars, velocity, diffusivity, diff_scale, basis_old, sing_values, stored):
    coeffs = jnp.concatenate([velocity, diffusivity[None]], 0)
    coeff_pad = jnp.pad(coeffs, ((0, 0), (2, 2), (2, 2), (0, 0)), mode='wrap')

    def advance(fields):

        def single(pair):
            padded = jnp.pad(pair[0][None], ((0, 0), (2, 2), (2, 2), (0, 0)), mode='wrap')
            return tendency(padded, coeff_pad, pair[1][None])[0]
        return lax.map(single, (fields, diff_scale))
    middle = advance(scalars)
    result = advance(middle)
    half_x = result.shape[1] // 2
    fresh = result[0, ::2, ::2, ::2].reshape(1, -1)
    rank = basis_old.shape[0]
    static = jnp.concatenate([basis_old.reshape(rank, -1).astype(jnp.float32) * sing_values[:, None], stored.reshape(stored.shape[0], -1).astype(jnp.float32)], 0)
    columns = jnp.concatenate([static, fresh], 0)
    gram = jnp.dot(columns, columns.T, precision=lax.Precision.HIGHEST) / columns.shape[1]
    lower = jnp.linalg.cholesky(gram)
    identity = jnp.eye(columns.shape[0], dtype=jnp.float32)
    inverse = lax.linalg.triangular_solve(lower, identity, left_side=True, lower=True)
    basis_new = jnp.dot(inverse, columns, precision=lax.Precision.HIGHEST).reshape(columns.shape[0], half_x, -1)
    return (result, basis_new, lower.T)
```

```python
import jax
import jax.numpy as jnp
from jax import lax
from jax.sharding import PartitionSpec as P

time_step = 0.25


def padded_2(block, sides, width):
    for axis, dim in sides:
        count = lax.axis_size(axis)
        forward = [(i, i + 1) for i in range(count - 1)]
        forward.append((count - 1, 0))
        backward = [(target, source) for source, target in forward]
        low = lax.ppermute(
            lax.slice_in_dim(block, block.shape[dim] - width, None, axis=dim), axis, forward
        )
        high = lax.ppermute(lax.slice_in_dim(block, 0, width, axis=dim), axis, backward)
        block = jnp.concatenate([low, block, high], axis=dim)
    return block


def tendency(concen, coeffs, diff_scale):
    velocity = coeffs[:3]
    kappa = coeffs[3]
    center = concen[:, 2:-2, 2:-2, :]
    flux_first = velocity[0][None] * concen
    slope = (
        8.0 * (flux_first[:, 3:-1, 2:-2] - flux_first[:, 1:-3, 2:-2])
        - (flux_first[:, 4:, 2:-2] - flux_first[:, :-4, 2:-2])
    ) / 12.0
    flux_second = velocity[1][None] * concen
    slope = (
        slope
        + (
            8.0 * (flux_second[:, 2:-2, 3:-1] - flux_second[:, 2:-2, 1:-3])
            - (flux_second[:, 2:-2, 4:] - flux_second[:, 2:-2, :-4])
        )
        / 12.0
    )
    flux_third = jnp.pad(velocity[2][2:-2, 2:-2][None] * center, ((0, 0), (0, 0), (0, 0), (2, 2)))
    slope = (
        slope
        + (
            8.0 * (flux_third[..., 3:-1] - flux_third[..., 1:-3])
            - (flux_third[..., 4:] - flux_third[..., :-4])
        )
        / 12.0
    )
    kappa_mid = kappa[2:-2, 2:-2][None]
    spread = (kappa_mid + kappa[3:-1, 2:-2][None]) * 0.5 * (concen[:, 3:-1, 2:-2] - center) - (
        kappa_mid + kappa[1:-3, 2:-2][None]
    ) * 0.5 * (center - concen[:, 1:-3, 2:-2])
    spread = (
        spread
        + (kappa_mid + kappa[2:-2, 3:-1][None]) * 0.5 * (concen[:, 2:-2, 3:-1] - center)
        - (kappa_mid + kappa[2:-2, 1:-3][None]) * 0.5 * (center - concen[:, 2:-2, 1:-3])
    )
    kappa_pad = jnp.pad(kappa_mid, ((0, 0), (0, 0), (0, 0), (1, 1)))
    center_pad = jnp.pad(center, ((0, 0), (0, 0), (0, 0), (1, 1)))
    spread = (
        spread
        + (kappa_mid + kappa_pad[..., 2:]) * 0.5 * (center_pad[..., 2:] - center)
        - (kappa_mid + kappa_pad[..., :-2]) * 0.5 * (center - center_pad[..., :-2])
    )
    return center + time_step * (diff_scale[:, None, None, None] * spread - slope)


def butterfly_sum(value):
    for axis in ("gx", "gy"):
        count = lax.axis_size(axis)
        bit = 1
        while bit < count:
            pairs = [(i, i ^ bit) for i in range(count)]
            value = value + lax.ppermute(value, axis, pairs)
            bit *= 2
    return value


def halo(block):
    return padded_2(block, (("gx", 1), ("gy", 2)), 2)


def per_device(scalars, velocity, diffusivity, diff_scale, basis_old, sing_values, stored):
    rank = basis_old.shape[0]
    snaps = stored.shape[0]
    static = jnp.concatenate([basis_old, stored], 0)
    weight = jnp.concatenate([sing_values, jnp.ones((snaps,), jnp.float32)], 0)
    total_rows = static.shape[1] * static.shape[2] * lax.axis_size("gx") * lax.axis_size("gy")

    local_gram = lax.dot_general(
        static, static, (((1, 2), (1, 2)), ((), ())), preferred_element_type=jnp.float32
    )
    gram_static = butterfly_sum(local_gram) * (weight[:, None] * weight[None, :]) / total_rows
    lower_static = jnp.linalg.cholesky(gram_static)
    width = rank + snaps
    inv_static = lax.linalg.triangular_solve(
        lower_static, jnp.eye(width, dtype=jnp.float32), left_side=True, lower=True
    )
    mix = inv_static * weight[None, :]
    mix_ext = jnp.concatenate([mix, jnp.zeros((1, width), jnp.float32)], 0)
    basis_ext = lax.dot_general(
        mix_ext,
        static.astype(jnp.float32),
        (((1,), (0,)), ((), ())),
        precision=lax.Precision.HIGHEST,
    )

    coeffs = jnp.concatenate([velocity, diffusivity[None]], 0)
    first = halo(jnp.concatenate([scalars[:1], coeffs], 0))
    coeff_pad = first[1:]
    middle0 = tendency(first[:1], coeff_pad, diff_scale[:1])
    result0 = tendency(halo(middle0), coeff_pad, diff_scale[:1])

    fresh = result0[0, ::2, ::2, ::2].reshape(result0.shape[1] // 2, -1)
    static_f32 = static.astype(jnp.float32)
    cross = jnp.sum(static_f32 * fresh[None], axis=(1, 2))
    self_dot = jnp.sum(fresh * fresh)
    moments = butterfly_sum(jnp.concatenate([cross, self_dot[None]], 0)) / total_rows
    cross_g = moments[:width] * weight
    self_g = moments[width]

    rest = halo(scalars[1:])
    middle_r = tendency(rest, coeff_pad, diff_scale[1:])
    result_r = tendency(halo(middle_r), coeff_pad, diff_scale[1:])
    result = jnp.concatenate([result0, result_r], 0)

    link = lax.linalg.triangular_solve(
        lower_static, cross_g[:, None], left_side=True, lower=True
    )[:, 0]
    corner = jnp.sqrt(self_g - jnp.sum(link * link))
    lower = jnp.zeros((width + 1, width + 1), jnp.float32)
    lower = lower.at[:width, :width].set(lower_static)
    lower = lower.at[width, :width].set(link)
    lower = lower.at[width, width].set(corner)

    along = jnp.sum(mix * link[:, None], axis=0)
    last = (fresh - jnp.sum(static_f32 * along[:, None, None], axis=0)) / corner
    basis_new = lax.dynamic_update_slice(basis_ext, last[None], (width, 0, 0))
    return (result, basis_new, lower.T)


def solution(mesh):
    return jax.shard_map(
        per_device,
        mesh=mesh,
        in_specs=(
            P(None, "gx", "gy", None),
            P(None, "gx", "gy", None),
            P("gx", "gy", None),
            P(),
            P(None, "gx", "gy"),
            P(),
            P(None, "gx", "gy"),
        ),
        out_specs=(P(None, "gx", "gy", None), P(None, "gx", "gy"), P()),
        check_vma=False,
    )
```

```python
import jax
import jax.numpy as jnp
from jax import lax
from jax.sharding import PartitionSpec as P
from jax.experimental import pallas as pl

time_step = 0.25


def ring(axis):
    count = lax.axis_size(axis)
    forward = [(i, (i + 1) % count) for i in range(count)]
    backward = [(target, source) for source, target in forward]
    return forward, backward


def halo(block, width=2):
    fx, bx = ring("gx")
    fy, by = ring("gy")
    nx, ny = block.shape[1], block.shape[2]
    low_x = lax.ppermute(block[:, nx - width :], "gx", fx)
    high_x = lax.ppermute(block[:, :width], "gx", bx)
    low_y = lax.ppermute(block[:, :, ny - width :], "gy", fy)
    high_y = lax.ppermute(block[:, :, :width], "gy", by)
    rows = jnp.concatenate([low_x, block, high_x], axis=1)
    edge = ((0, 0), (width, width), (0, 0), (0, 0))
    return jnp.concatenate([jnp.pad(low_y, edge), rows, jnp.pad(high_y, edge)], axis=2)


def butterfly_sum(value):
    for axis in ("gx", "gy"):
        count = lax.axis_size(axis)
        bit = 1
        while bit < count:
            pairs = [(i, i ^ bit) for i in range(count)]
            value = value + lax.ppermute(value, axis, pairs)
            bit *= 2
    return value


def put_last_row(basis_ext, last):
    def body(_, last_ref, out_ref):
        out_ref[...] = last_ref[...]

    row = basis_ext.shape[0] - 1
    return pl.pallas_call(
        body,
        out_shape=jax.ShapeDtypeStruct(basis_ext.shape, basis_ext.dtype),
        grid=(1,),
        in_specs=[pl.BlockSpec(memory_space=pl.ANY), pl.BlockSpec(last.shape, lambda i: (0, 0, 0))],
        out_specs=pl.BlockSpec(last.shape, lambda i: (row, 0, 0)),
        input_output_aliases={0: 0},
    )(basis_ext, last)


def tendency(concen, coeffs, diff_scale):
    velocity = coeffs[:3]
    kappa = coeffs[3]
    center = concen[:, 2:-2, 2:-2, :]
    flux_first = velocity[0][None] * concen
    slope = (
        8.0 * (flux_first[:, 3:-1, 2:-2] - flux_first[:, 1:-3, 2:-2])
        - (flux_first[:, 4:, 2:-2] - flux_first[:, :-4, 2:-2])
    ) / 12.0
    flux_second = velocity[1][None] * concen
    slope = (
        slope
        + (
            8.0 * (flux_second[:, 2:-2, 3:-1] - flux_second[:, 2:-2, 1:-3])
            - (flux_second[:, 2:-2, 4:] - flux_second[:, 2:-2, :-4])
        )
        / 12.0
    )
    flux_third = jnp.pad(velocity[2][2:-2, 2:-2][None] * center, ((0, 0), (0, 0), (0, 0), (2, 2)))
    slope = (
        slope
        + (
            8.0 * (flux_third[..., 3:-1] - flux_third[..., 1:-3])
            - (flux_third[..., 4:] - flux_third[..., :-4])
        )
        / 12.0
    )
    kappa_mid = kappa[2:-2, 2:-2][None]
    spread = (kappa_mid + kappa[3:-1, 2:-2][None]) * 0.5 * (concen[:, 3:-1, 2:-2] - center) - (
        kappa_mid + kappa[1:-3, 2:-2][None]
    ) * 0.5 * (center - concen[:, 1:-3, 2:-2])
    spread = (
        spread
        + (kappa_mid + kappa[2:-2, 3:-1][None]) * 0.5 * (concen[:, 2:-2, 3:-1] - center)
        - (kappa_mid + kappa[2:-2, 1:-3][None]) * 0.5 * (center - concen[:, 2:-2, 1:-3])
    )
    kappa_pad = jnp.pad(kappa_mid, ((0, 0), (0, 0), (0, 0), (1, 1)))
    center_pad = jnp.pad(center, ((0, 0), (0, 0), (0, 0), (1, 1)))
    spread = (
        spread
        + (kappa_mid + kappa_pad[..., 2:]) * 0.5 * (center_pad[..., 2:] - center)
        - (kappa_mid + kappa_pad[..., :-2]) * 0.5 * (center - center_pad[..., :-2])
    )
    return center + time_step * (diff_scale[:, None, None, None] * spread - slope)


def per_device(scalars, velocity, diffusivity, diff_scale, basis_old, sing_values, stored):
    rank = basis_old.shape[0]
    snaps = stored.shape[0]
    static = jnp.concatenate([basis_old, stored], 0)
    weight = jnp.concatenate([sing_values, jnp.ones((snaps,), jnp.float32)], 0)
    total_rows = static.shape[1] * static.shape[2] * lax.axis_size("gx") * lax.axis_size("gy")

    local_gram = lax.dot_general(
        static, static, (((1, 2), (1, 2)), ((), ())), preferred_element_type=jnp.float32
    )
    gram_static = butterfly_sum(local_gram) * (weight[:, None] * weight[None, :]) / total_rows
    lower_static = jnp.linalg.cholesky(gram_static)
    width = rank + snaps
    inv_static = lax.linalg.triangular_solve(
        lower_static, jnp.eye(width, dtype=jnp.float32), left_side=True, lower=True
    )
    mix = inv_static * weight[None, :]
    mix_ext = jnp.concatenate([mix, jnp.zeros((1, width), jnp.float32)], 0)
    basis_ext = lax.dot_general(
        mix_ext,
        static.astype(jnp.float32),
        (((1,), (0,)), ((), ())),
        precision=lax.Precision.HIGHEST,
    )

    coeffs = jnp.concatenate([velocity, diffusivity[None]], 0)
    first = halo(jnp.concatenate([scalars[:1], coeffs], 0))
    coeff_pad = first[1:]
    middle0 = tendency(first[:1], coeff_pad, diff_scale[:1])
    result0 = tendency(halo(middle0), coeff_pad, diff_scale[:1])

    coarse = result0[0, ::2]
    span, depth = coarse.shape[1], coarse.shape[2]
    pick_z = (jnp.arange(depth)[:, None] == 2 * jnp.arange(depth // 2)[None, :]).astype(jnp.float32)
    pick_y = (2 * jnp.arange(span // 2)[:, None] == jnp.arange(span)[None, :]).astype(jnp.float32)
    thin = jnp.einsum("ayz,zk->ayk", coarse, pick_z, precision=lax.Precision.HIGHEST)
    fresh = jnp.einsum("jy,ayk->ajk", pick_y, thin, precision=lax.Precision.HIGHEST).reshape(
        coarse.shape[0], -1
    )
    static_f32 = static.astype(jnp.float32)
    cross = jnp.sum(static_f32 * fresh[None], axis=(1, 2))
    self_dot = jnp.sum(fresh * fresh)
    moments = butterfly_sum(jnp.concatenate([cross, self_dot[None]], 0)) / total_rows
    cross_g = moments[:width] * weight
    self_g = moments[width]

    rest = halo(scalars[1:])
    middle_r = tendency(rest, coeff_pad, diff_scale[1:])
    result_r = tendency(halo(middle_r), coeff_pad, diff_scale[1:])
    result = jnp.concatenate([result0, result_r], 0)

    link = lax.linalg.triangular_solve(
        lower_static, cross_g[:, None], left_side=True, lower=True
    )[:, 0]
    corner = jnp.sqrt(self_g - jnp.sum(link * link))
    lower = jnp.zeros((width + 1, width + 1), jnp.float32)
    lower = lower.at[:width, :width].set(lower_static)
    lower = lower.at[width, :width].set(link)
    lower = lower.at[width, width].set(corner)

    along = jnp.sum(mix * link[:, None], axis=0)
    last = (fresh - jnp.sum(static_f32 * along[:, None, None], axis=0)) / corner
    basis_new = put_last_row(basis_ext, last.reshape((1,) + basis_ext.shape[1:]))
    return (result, basis_new, lower.T)


def solution(mesh):
    return jax.shard_map(
        per_device,
        mesh=mesh,
        in_specs=(
            P(None, "gx", "gy", None),
            P(None, "gx", "gy", None),
            P("gx", "gy", None),
            P(),
            P(None, "gx", "gy"),
            P(),
            P(None, "gx", "gy"),
        ),
        out_specs=(P(None, "gx", "gy", None), P(None, "gx", "gy"), P()),
        check_vma=False,
    )
```

```python
import jax
import jax.numpy as jnp
from jax import lax
from jax.sharding import PartitionSpec as P
from jax.experimental import pallas as pl
from jax.experimental.pallas import tpu as pltpu

time_step = 0.25


def ring(axis):
    count = lax.axis_size(axis)
    forward = [(i, (i + 1) % count) for i in range(count)]
    backward = [(target, source) for source, target in forward]
    return forward, backward


def halo(block, width=2):
    fx, bx = ring("gx")
    fy, by = ring("gy")
    nx, ny = block.shape[1], block.shape[2]
    low_x = lax.ppermute(block[:, nx - width :], "gx", fx)
    high_x = lax.ppermute(block[:, :width], "gx", bx)
    low_y = lax.ppermute(block[:, :, ny - width :], "gy", fy)
    high_y = lax.ppermute(block[:, :, :width], "gy", by)
    rows = jnp.concatenate([low_x, block, high_x], axis=1)
    edge = ((0, 0), (width, width), (0, 0), (0, 0))
    return jnp.concatenate([jnp.pad(low_y, edge), rows, jnp.pad(high_y, edge)], axis=2)


def butterfly_sum(value):
    for axis in ("gx", "gy"):
        count = lax.axis_size(axis)
        bit = 1
        while bit < count:
            pairs = [(i, i ^ bit) for i in range(count)]
            value = value + lax.ppermute(value, axis, pairs)
            bit *= 2
    return value


def put_last_row(basis_ext, last):
    def body(_, last_ref, out_ref):
        out_ref[...] = last_ref[...]

    row = basis_ext.shape[0] - 1
    return pl.pallas_call(
        body,
        out_shape=jax.ShapeDtypeStruct(basis_ext.shape, basis_ext.dtype),
        grid=(1,),
        in_specs=[pl.BlockSpec(memory_space=pl.ANY), pl.BlockSpec(last.shape, lambda i: (0, 0, 0))],
        out_specs=pl.BlockSpec(last.shape, lambda i: (row, 0, 0)),
        input_output_aliases={0: 0},
    )(basis_ext, last)


def tendency(concen, coeffs, diff_scale):
    velocity = coeffs[:3]
    kappa = coeffs[3]
    center = concen[:, 2:-2, 2:-2, :]
    flux_first = velocity[0][None] * concen
    slope = (
        8.0 * (flux_first[:, 3:-1, 2:-2] - flux_first[:, 1:-3, 2:-2])
        - (flux_first[:, 4:, 2:-2] - flux_first[:, :-4, 2:-2])
    ) / 12.0
    flux_second = velocity[1][None] * concen
    slope = (
        slope
        + (
            8.0 * (flux_second[:, 2:-2, 3:-1] - flux_second[:, 2:-2, 1:-3])
            - (flux_second[:, 2:-2, 4:] - flux_second[:, 2:-2, :-4])
        )
        / 12.0
    )
    flux_third = jnp.pad(velocity[2][2:-2, 2:-2][None] * center, ((0, 0), (0, 0), (0, 0), (2, 2)))
    slope = (
        slope
        + (
            8.0 * (flux_third[..., 3:-1] - flux_third[..., 1:-3])
            - (flux_third[..., 4:] - flux_third[..., :-4])
        )
        / 12.0
    )
    kappa_mid = kappa[2:-2, 2:-2][None]
    spread = (kappa_mid + kappa[3:-1, 2:-2][None]) * 0.5 * (concen[:, 3:-1, 2:-2] - center) - (
        kappa_mid + kappa[1:-3, 2:-2][None]
    ) * 0.5 * (center - concen[:, 1:-3, 2:-2])
    spread = (
        spread
        + (kappa_mid + kappa[2:-2, 3:-1][None]) * 0.5 * (concen[:, 2:-2, 3:-1] - center)
        - (kappa_mid + kappa[2:-2, 1:-3][None]) * 0.5 * (center - concen[:, 2:-2, 1:-3])
    )
    kappa_pad = jnp.pad(kappa_mid, ((0, 0), (0, 0), (0, 0), (1, 1)))
    center_pad = jnp.pad(center, ((0, 0), (0, 0), (0, 0), (1, 1)))
    spread = (
        spread
        + (kappa_mid + kappa_pad[..., 2:]) * 0.5 * (center_pad[..., 2:] - center)
        - (kappa_mid + kappa_pad[..., :-2]) * 0.5 * (center - center_pad[..., :-2])
    )
    return center + time_step * (diff_scale[:, None, None, None] * spread - slope)


def stencil_body(scale_ref, conc_ref, coeff_ref, out_ref):
    s = pl.program_id(0)
    scale = scale_ref[s]
    rows = out_ref.shape[2]
    depth = out_ref.shape[3]
    lane = lax.broadcasted_iota(jnp.int32, (rows, depth), 1)

    def shifted(value, d):
        rolled = pltpu.roll(value, (-d) % depth, 1)
        keep = (lane + d >= 0) & (lane + d < depth)
        return jnp.where(keep, rolled, 0.0)

    def row(i, carry):
        def c(dx, dy):
            return conc_ref[0, i + 2 + dx, pl.ds(2 + dy, rows), :]

        def k(field, dx, dy):
            return coeff_ref[field, i + 2 + dx, pl.ds(2 + dy, rows), :]

        center = c(0, 0)

        def f1(d):
            return k(0, d, 0) * c(d, 0)

        slope = (8.0 * (f1(1) - f1(-1)) - (f1(2) - f1(-2))) / 12.0

        def f2(d):
            return k(1, 0, d) * c(0, d)

        slope = slope + (8.0 * (f2(1) - f2(-1)) - (f2(2) - f2(-2))) / 12.0
        f3 = k(2, 0, 0) * center
        slope = slope + (
            8.0 * (shifted(f3, 1) - shifted(f3, -1)) - (shifted(f3, 2) - shifted(f3, -2))
        ) / 12.0
        kmid = k(3, 0, 0)
        spread = (kmid + k(3, 1, 0)) * 0.5 * (c(1, 0) - center) - (kmid + k(3, -1, 0)) * 0.5 * (
            center - c(-1, 0)
        )
        spread = (
            spread
            + (kmid + k(3, 0, 1)) * 0.5 * (c(0, 1) - center)
            - (kmid + k(3, 0, -1)) * 0.5 * (center - c(0, -1))
        )
        spread = (
            spread
            + (kmid + shifted(kmid, 1)) * 0.5 * (shifted(center, 1) - center)
            - (kmid + shifted(kmid, -1)) * 0.5 * (center - shifted(center, -1))
        )
        out_ref[0, i] = center + time_step * (scale * spread - slope)
        return carry

    lax.fori_loop(0, out_ref.shape[1], row, 0)


def stencil_step(conc_pad, coeff_pad, scale):
    count, px, py, depth = conc_pad.shape
    nx, ny = px - 4, py - 4
    return pl.pallas_call(
        stencil_body,
        out_shape=jax.ShapeDtypeStruct((count, nx, ny, depth), jnp.float32),
        grid=(count,),
        in_specs=[
            pl.BlockSpec(memory_space=pltpu.SMEM),
            pl.BlockSpec((1, px, py, depth), lambda s: (s, 0, 0, 0)),
            pl.BlockSpec(coeff_pad.shape, lambda s: (0, 0, 0, 0)),
        ],
        out_specs=pl.BlockSpec((1, nx, ny, depth), lambda s: (s, 0, 0, 0)),
        compiler_params=pltpu.CompilerParams(vmem_limit_bytes=48 * 1024 * 1024),
        cost_estimate=pl.CostEstimate(
            flops=80 * count * nx * ny * depth,
            transcendentals=0,
            bytes_accessed=4 * (conc_pad.size + coeff_pad.size + count * nx * ny * depth),
        ),
    )(scale, conc_pad, coeff_pad)


def per_device(scalars, velocity, diffusivity, diff_scale, basis_old, sing_values, stored):
    rank = basis_old.shape[0]
    snaps = stored.shape[0]
    static = jnp.concatenate([basis_old, stored], 0)
    weight = jnp.concatenate([sing_values, jnp.ones((snaps,), jnp.float32)], 0)
    total_rows = static.shape[1] * static.shape[2] * lax.axis_size("gx") * lax.axis_size("gy")

    local_gram = lax.dot_general(
        static, static, (((1, 2), (1, 2)), ((), ())), preferred_element_type=jnp.float32
    )
    gram_static = butterfly_sum(local_gram) * (weight[:, None] * weight[None, :]) / total_rows
    lower_static = jnp.linalg.cholesky(gram_static)
    width = rank + snaps
    inv_static = lax.linalg.triangular_solve(
        lower_static, jnp.eye(width, dtype=jnp.float32), left_side=True, lower=True
    )
    mix = inv_static * weight[None, :]
    mix_ext = jnp.concatenate([mix, jnp.zeros((1, width), jnp.float32)], 0)
    basis_ext = lax.dot_general(
        mix_ext,
        static.astype(jnp.float32),
        (((1,), (0,)), ((), ())),
        precision=lax.Precision.HIGHEST,
    )

    coeffs = jnp.concatenate([velocity, diffusivity[None]], 0)
    first = halo(jnp.concatenate([scalars[:1], coeffs], 0))
    coeff_pad = first[1:]
    middle0 = stencil_step(first[:1], coeff_pad, diff_scale[:1])
    result0 = stencil_step(halo(middle0), coeff_pad, diff_scale[:1])

    coarse = result0[0, ::2]
    span, depth = coarse.shape[1], coarse.shape[2]
    pick_z = (jnp.arange(depth)[:, None] == 2 * jnp.arange(depth // 2)[None, :]).astype(jnp.float32)
    pick_y = (2 * jnp.arange(span // 2)[:, None] == jnp.arange(span)[None, :]).astype(jnp.float32)
    thin = jnp.einsum("ayz,zk->ayk", coarse, pick_z, precision=lax.Precision.HIGHEST)
    fresh = jnp.einsum("jy,ayk->ajk", pick_y, thin, precision=lax.Precision.HIGHEST).reshape(
        coarse.shape[0], -1
    )
    static_f32 = static.astype(jnp.float32)
    cross = jnp.sum(static_f32 * fresh[None], axis=(1, 2))
    self_dot = jnp.sum(fresh * fresh)
    moments = butterfly_sum(jnp.concatenate([cross, self_dot[None]], 0)) / total_rows
    cross_g = moments[:width] * weight
    self_g = moments[width]

    rest = halo(scalars[1:])
    middle_r = stencil_step(rest, coeff_pad, diff_scale[1:])
    result_r = stencil_step(halo(middle_r), coeff_pad, diff_scale[1:])
    result = jnp.concatenate([result0, result_r], 0)

    link = lax.linalg.triangular_solve(
        lower_static, cross_g[:, None], left_side=True, lower=True
    )[:, 0]
    corner = jnp.sqrt(self_g - jnp.sum(link * link))
    lower = jnp.zeros((width + 1, width + 1), jnp.float32)
    lower = lower.at[:width, :width].set(lower_static)
    lower = lower.at[width, :width].set(link)
    lower = lower.at[width, width].set(corner)

    along = jnp.sum(mix * link[:, None], axis=0)
    last = (fresh - jnp.sum(static_f32 * along[:, None, None], axis=0)) / corner
    basis_new = put_last_row(basis_ext, last.reshape((1,) + basis_ext.shape[1:]))
    return (result, basis_new, lower.T)


def solution(mesh):
    return jax.shard_map(
        per_device,
        mesh=mesh,
        in_specs=(
            P(None, "gx", "gy", None),
            P(None, "gx", "gy", None),
            P("gx", "gy", None),
            P(),
            P(None, "gx", "gy"),
            P(),
            P(None, "gx", "gy"),
        ),
        out_specs=(P(None, "gx", "gy", None), P(None, "gx", "gy"), P()),
        check_vma=False,
    )
```

```python
import jax
import jax.numpy as jnp
from jax import lax
from jax.sharding import PartitionSpec as P
from jax.experimental import pallas as pl
from jax.experimental.pallas import tpu as pltpu

time_step = 0.25


def ring(axis):
    count = lax.axis_size(axis)
    forward = [(i, (i + 1) % count) for i in range(count)]
    backward = [(target, source) for source, target in forward]
    return forward, backward


def halo(block, width=2):
    fx, bx = ring("gx")
    fy, by = ring("gy")
    nx, ny = block.shape[1], block.shape[2]
    low_x = lax.ppermute(block[:, nx - width :], "gx", fx)
    high_x = lax.ppermute(block[:, :width], "gx", bx)
    low_y = lax.ppermute(block[:, :, ny - width :], "gy", fy)
    high_y = lax.ppermute(block[:, :, :width], "gy", by)
    rows = jnp.concatenate([low_x, block, high_x], axis=1)
    edge = ((0, 0), (width, width), (0, 0), (0, 0))
    return jnp.concatenate([jnp.pad(low_y, edge), rows, jnp.pad(high_y, edge)], axis=2)


def butterfly_sum(value):
    for axis in ("gx", "gy"):
        count = lax.axis_size(axis)
        bit = 1
        while bit < count:
            pairs = [(i, i ^ bit) for i in range(count)]
            value = value + lax.ppermute(value, axis, pairs)
            bit *= 2
    return value


def put_last_row(basis_ext, last):
    def body(_, last_ref, out_ref):
        out_ref[...] = last_ref[...]

    row = basis_ext.shape[0] - 1
    return pl.pallas_call(
        body,
        out_shape=jax.ShapeDtypeStruct(basis_ext.shape, basis_ext.dtype),
        grid=(1,),
        in_specs=[pl.BlockSpec(memory_space=pl.ANY), pl.BlockSpec(last.shape, lambda i: (0, 0, 0))],
        out_specs=pl.BlockSpec(last.shape, lambda i: (row, 0, 0)),
        input_output_aliases={0: 0},
    )(basis_ext, last)


def tendency(concen, coeffs, diff_scale):
    velocity = coeffs[:3]
    kappa = coeffs[3]
    center = concen[:, 2:-2, 2:-2, :]
    flux_first = velocity[0][None] * concen
    slope = (
        8.0 * (flux_first[:, 3:-1, 2:-2] - flux_first[:, 1:-3, 2:-2])
        - (flux_first[:, 4:, 2:-2] - flux_first[:, :-4, 2:-2])
    ) / 12.0
    flux_second = velocity[1][None] * concen
    slope = (
        slope
        + (
            8.0 * (flux_second[:, 2:-2, 3:-1] - flux_second[:, 2:-2, 1:-3])
            - (flux_second[:, 2:-2, 4:] - flux_second[:, 2:-2, :-4])
        )
        / 12.0
    )
    flux_third = jnp.pad(velocity[2][2:-2, 2:-2][None] * center, ((0, 0), (0, 0), (0, 0), (2, 2)))
    slope = (
        slope
        + (
            8.0 * (flux_third[..., 3:-1] - flux_third[..., 1:-3])
            - (flux_third[..., 4:] - flux_third[..., :-4])
        )
        / 12.0
    )
    kappa_mid = kappa[2:-2, 2:-2][None]
    spread = (kappa_mid + kappa[3:-1, 2:-2][None]) * 0.5 * (concen[:, 3:-1, 2:-2] - center) - (
        kappa_mid + kappa[1:-3, 2:-2][None]
    ) * 0.5 * (center - concen[:, 1:-3, 2:-2])
    spread = (
        spread
        + (kappa_mid + kappa[2:-2, 3:-1][None]) * 0.5 * (concen[:, 2:-2, 3:-1] - center)
        - (kappa_mid + kappa[2:-2, 1:-3][None]) * 0.5 * (center - concen[:, 2:-2, 1:-3])
    )
    kappa_pad = jnp.pad(kappa_mid, ((0, 0), (0, 0), (0, 0), (1, 1)))
    center_pad = jnp.pad(center, ((0, 0), (0, 0), (0, 0), (1, 1)))
    spread = (
        spread
        + (kappa_mid + kappa_pad[..., 2:]) * 0.5 * (center_pad[..., 2:] - center)
        - (kappa_mid + kappa_pad[..., :-2]) * 0.5 * (center - center_pad[..., :-2])
    )
    return center + time_step * (diff_scale[:, None, None, None] * spread - slope)


def stencil_body(scale_ref, conc_ref, coeff_ref, out_ref):
    s = pl.program_id(0)
    scale = scale_ref[s]
    rows = out_ref.shape[2]
    depth = out_ref.shape[3]
    lane = lax.broadcasted_iota(jnp.int32, (rows, depth), 1)

    def shifted(value, d):
        rolled = pltpu.roll(value, (-d) % depth, 1)
        keep = (lane + d >= 0) & (lane + d < depth)
        return jnp.where(keep, rolled, 0.0)

    def row(i, carry):
        def c(dx, dy):
            return conc_ref[0, i + 2 + dx, pl.ds(2 + dy, rows), :]

        def k(field, dx, dy):
            return coeff_ref[field, i + 2 + dx, pl.ds(2 + dy, rows), :]

        center = c(0, 0)

        def f1(d):
            return k(0, d, 0) * c(d, 0)

        slope = (8.0 * (f1(1) - f1(-1)) - (f1(2) - f1(-2))) / 12.0

        def f2(d):
            return k(1, 0, d) * c(0, d)

        slope = slope + (8.0 * (f2(1) - f2(-1)) - (f2(2) - f2(-2))) / 12.0
        f3 = k(2, 0, 0) * center
        slope = slope + (
            8.0 * (shifted(f3, 1) - shifted(f3, -1)) - (shifted(f3, 2) - shifted(f3, -2))
        ) / 12.0
        kmid = k(3, 0, 0)
        spread = (kmid + k(3, 1, 0)) * 0.5 * (c(1, 0) - center) - (kmid + k(3, -1, 0)) * 0.5 * (
            center - c(-1, 0)
        )
        spread = (
            spread
            + (kmid + k(3, 0, 1)) * 0.5 * (c(0, 1) - center)
            - (kmid + k(3, 0, -1)) * 0.5 * (center - c(0, -1))
        )
        spread = (
            spread
            + (kmid + shifted(kmid, 1)) * 0.5 * (shifted(center, 1) - center)
            - (kmid + shifted(kmid, -1)) * 0.5 * (center - shifted(center, -1))
        )
        out_ref[0, i] = center + time_step * (scale * spread - slope)
        return carry

    lax.fori_loop(0, out_ref.shape[1], row, 0)


def stencil_step(conc_pad, coeff_pad, scale):
    count, px, py, depth = conc_pad.shape
    nx, ny = px - 4, py - 4
    return pl.pallas_call(
        stencil_body,
        out_shape=jax.ShapeDtypeStruct((count, nx, ny, depth), jnp.float32),
        grid=(count,),
        in_specs=[
            pl.BlockSpec(memory_space=pltpu.SMEM),
            pl.BlockSpec((1, px, py, depth), lambda s: (s, 0, 0, 0)),
            pl.BlockSpec(coeff_pad.shape, lambda s: (0, 0, 0, 0)),
        ],
        out_specs=pl.BlockSpec((1, nx, ny, depth), lambda s: (s, 0, 0, 0)),
        compiler_params=pltpu.CompilerParams(vmem_limit_bytes=48 * 1024 * 1024),
        cost_estimate=pl.CostEstimate(
            flops=80 * count * nx * ny * depth,
            transcendentals=0,
            bytes_accessed=4 * (conc_pad.size + coeff_pad.size + count * nx * ny * depth),
        ),
    )(scale, conc_pad, coeff_pad)


def basis_body(mix_ref, xt_ref, out_ref):
    for a in range(xt_ref.shape[0]):
        xa = xt_ref[a]
        res = jnp.dot(mix_ref[0], xa, preferred_element_type=jnp.float32)
        res = res + jnp.dot(mix_ref[1], xa, preferred_element_type=jnp.float32)
        res = res + jnp.dot(mix_ref[2], xa, preferred_element_type=jnp.float32)
        out_ref[:, a, :] = res


def basis_rows(mix_ext, static):
    hi = lax.reduce_precision(mix_ext, exponent_bits=8, mantissa_bits=7)
    rem = mix_ext - hi
    mid = lax.reduce_precision(rem, exponent_bits=8, mantissa_bits=7)
    lo = rem - mid
    parts = jnp.stack([hi, mid, lo], 0).astype(jnp.bfloat16)
    xt = jnp.transpose(static, (1, 0, 2))
    span, width, cols = xt.shape
    rows = mix_ext.shape[0]
    block = 8
    return pl.pallas_call(
        basis_body,
        out_shape=jax.ShapeDtypeStruct((rows, span, cols), jnp.float32),
        grid=(span // block,),
        in_specs=[
            pl.BlockSpec(parts.shape, lambda i: (0, 0, 0)),
            pl.BlockSpec((block, width, cols), lambda i: (i, 0, 0)),
        ],
        out_specs=pl.BlockSpec((rows, block, cols), lambda i: (0, i, 0)),
        compiler_params=pltpu.CompilerParams(vmem_limit_bytes=48 * 1024 * 1024),
        cost_estimate=pl.CostEstimate(
            flops=6 * rows * width * span * cols,
            transcendentals=0,
            bytes_accessed=2 * xt.size + 4 * rows * span * cols,
        ),
    )(parts, xt)


def per_device(scalars, velocity, diffusivity, diff_scale, basis_old, sing_values, stored):
    rank = basis_old.shape[0]
    snaps = stored.shape[0]
    static = jnp.concatenate([basis_old, stored], 0)
    weight = jnp.concatenate([sing_values, jnp.ones((snaps,), jnp.float32)], 0)
    total_rows = static.shape[1] * static.shape[2] * lax.axis_size("gx") * lax.axis_size("gy")

    local_gram = lax.dot_general(
        static, static, (((1, 2), (1, 2)), ((), ())), preferred_element_type=jnp.float32
    )
    gram_static = butterfly_sum(local_gram) * (weight[:, None] * weight[None, :]) / total_rows
    lower_static = jnp.linalg.cholesky(gram_static)
    width = rank + snaps
    inv_static = lax.linalg.triangular_solve(
        lower_static, jnp.eye(width, dtype=jnp.float32), left_side=True, lower=True
    )
    mix = inv_static * weight[None, :]
    mix_ext = jnp.concatenate([mix, jnp.zeros((1, width), jnp.float32)], 0)
    basis_ext = basis_rows(mix_ext, static)

    coeffs = jnp.concatenate([velocity, diffusivity[None]], 0)
    first = halo(jnp.concatenate([scalars[:1], coeffs], 0))
    coeff_pad = first[1:]
    middle0 = stencil_step(first[:1], coeff_pad, diff_scale[:1])
    result0 = stencil_step(halo(middle0), coeff_pad, diff_scale[:1])

    coarse = result0[0, ::2]
    span, depth = coarse.shape[1], coarse.shape[2]
    pick_z = (jnp.arange(depth)[:, None] == 2 * jnp.arange(depth // 2)[None, :]).astype(jnp.float32)
    pick_y = (2 * jnp.arange(span // 2)[:, None] == jnp.arange(span)[None, :]).astype(jnp.float32)
    thin = jnp.einsum("ayz,zk->ayk", coarse, pick_z, precision=lax.Precision.HIGHEST)
    fresh = jnp.einsum("jy,ayk->ajk", pick_y, thin, precision=lax.Precision.HIGHEST).reshape(
        coarse.shape[0], -1
    )
    static_f32 = static.astype(jnp.float32)
    cross = jnp.sum(static_f32 * fresh[None], axis=(1, 2))
    self_dot = jnp.sum(fresh * fresh)
    moments = butterfly_sum(jnp.concatenate([cross, self_dot[None]], 0)) / total_rows
    cross_g = moments[:width] * weight
    self_g = moments[width]

    rest = halo(scalars[1:])
    middle_r = stencil_step(rest, coeff_pad, diff_scale[1:])
    result_r = stencil_step(halo(middle_r), coeff_pad, diff_scale[1:])
    result = jnp.concatenate([result0, result_r], 0)

    link = lax.linalg.triangular_solve(
        lower_static, cross_g[:, None], left_side=True, lower=True
    )[:, 0]
    corner = jnp.sqrt(self_g - jnp.sum(link * link))
    lower = jnp.zeros((width + 1, width + 1), jnp.float32)
    lower = lower.at[:width, :width].set(lower_static)
    lower = lower.at[width, :width].set(link)
    lower = lower.at[width, width].set(corner)

    along = jnp.sum(mix * link[:, None], axis=0)
    last = (fresh - jnp.sum(static_f32 * along[:, None, None], axis=0)) / corner
    basis_new = put_last_row(basis_ext, last.reshape((1,) + basis_ext.shape[1:]))
    return (result, basis_new, lower.T)


def solution(mesh):
    return jax.shard_map(
        per_device,
        mesh=mesh,
        in_specs=(
            P(None, "gx", "gy", None),
            P(None, "gx", "gy", None),
            P("gx", "gy", None),
            P(),
            P(None, "gx", "gy"),
            P(),
            P(None, "gx", "gy"),
        ),
        out_specs=(P(None, "gx", "gy", None), P(None, "gx", "gy"), P()),
        check_vma=False,
    )
```

```python
import jax
import jax.numpy as jnp
from jax import lax
from jax.sharding import PartitionSpec as P
from jax.experimental import pallas as pl
from jax.experimental.pallas import tpu as pltpu

time_step = 0.25


def ring(axis):
    count = lax.axis_size(axis)
    forward = [(i, (i + 1) % count) for i in range(count)]
    backward = [(target, source) for source, target in forward]
    return forward, backward


def halo(block, width=2):
    fx, bx = ring("gx")
    fy, by = ring("gy")
    nx, ny = block.shape[1], block.shape[2]
    low_x = lax.ppermute(block[:, nx - width :], "gx", fx)
    high_x = lax.ppermute(block[:, :width], "gx", bx)
    low_y = lax.ppermute(block[:, :, ny - width :], "gy", fy)
    high_y = lax.ppermute(block[:, :, :width], "gy", by)
    rows = jnp.concatenate([low_x, block, high_x], axis=1)
    edge = ((0, 0), (width, width), (0, 0), (0, 0))
    return jnp.concatenate([jnp.pad(low_y, edge), rows, jnp.pad(high_y, edge)], axis=2)


def butterfly_sum(value):
    for axis in ("gx", "gy"):
        count = lax.axis_size(axis)
        bit = 1
        while bit < count:
            pairs = [(i, i ^ bit) for i in range(count)]
            value = value + lax.ppermute(value, axis, pairs)
            bit *= 2
    return value


def put_last_row(basis_ext, last):
    def body(_, last_ref, out_ref):
        out_ref[...] = last_ref[...]

    row = basis_ext.shape[0] - 1
    return pl.pallas_call(
        body,
        out_shape=jax.ShapeDtypeStruct(basis_ext.shape, basis_ext.dtype),
        grid=(1,),
        in_specs=[pl.BlockSpec(memory_space=pl.ANY), pl.BlockSpec(last.shape, lambda i: (0, 0, 0))],
        out_specs=pl.BlockSpec(last.shape, lambda i: (row, 0, 0)),
        input_output_aliases={0: 0},
    )(basis_ext, last)


def tendency(concen, coeffs, diff_scale):
    velocity = coeffs[:3]
    kappa = coeffs[3]
    center = concen[:, 2:-2, 2:-2, :]
    flux_first = velocity[0][None] * concen
    slope = (
        8.0 * (flux_first[:, 3:-1, 2:-2] - flux_first[:, 1:-3, 2:-2])
        - (flux_first[:, 4:, 2:-2] - flux_first[:, :-4, 2:-2])
    ) / 12.0
    flux_second = velocity[1][None] * concen
    slope = (
        slope
        + (
            8.0 * (flux_second[:, 2:-2, 3:-1] - flux_second[:, 2:-2, 1:-3])
            - (flux_second[:, 2:-2, 4:] - flux_second[:, 2:-2, :-4])
        )
        / 12.0
    )
    flux_third = jnp.pad(velocity[2][2:-2, 2:-2][None] * center, ((0, 0), (0, 0), (0, 0), (2, 2)))
    slope = (
        slope
        + (
            8.0 * (flux_third[..., 3:-1] - flux_third[..., 1:-3])
            - (flux_third[..., 4:] - flux_third[..., :-4])
        )
        / 12.0
    )
    kappa_mid = kappa[2:-2, 2:-2][None]
    spread = (kappa_mid + kappa[3:-1, 2:-2][None]) * 0.5 * (concen[:, 3:-1, 2:-2] - center) - (
        kappa_mid + kappa[1:-3, 2:-2][None]
    ) * 0.5 * (center - concen[:, 1:-3, 2:-2])
    spread = (
        spread
        + (kappa_mid + kappa[2:-2, 3:-1][None]) * 0.5 * (concen[:, 2:-2, 3:-1] - center)
        - (kappa_mid + kappa[2:-2, 1:-3][None]) * 0.5 * (center - concen[:, 2:-2, 1:-3])
    )
    kappa_pad = jnp.pad(kappa_mid, ((0, 0), (0, 0), (0, 0), (1, 1)))
    center_pad = jnp.pad(center, ((0, 0), (0, 0), (0, 0), (1, 1)))
    spread = (
        spread
        + (kappa_mid + kappa_pad[..., 2:]) * 0.5 * (center_pad[..., 2:] - center)
        - (kappa_mid + kappa_pad[..., :-2]) * 0.5 * (center - center_pad[..., :-2])
    )
    return center + time_step * (diff_scale[:, None, None, None] * spread - slope)


def stencil_body(scale_ref, conc_ref, coeff_ref, out_ref):
    s = pl.program_id(0)
    scale = scale_ref[s]
    rows = out_ref.shape[2]
    depth = out_ref.shape[3]
    lane = lax.broadcasted_iota(jnp.int32, (rows, depth), 1)

    def shifted(value, d):
        rolled = pltpu.roll(value, (-d) % depth, 1)
        keep = (lane + d >= 0) & (lane + d < depth)
        return jnp.where(keep, rolled, 0.0)

    def row(i, carry):
        def c(dx, dy):
            return conc_ref[0, i + 2 + dx, pl.ds(2 + dy, rows), :]

        def k(field, dx, dy):
            return coeff_ref[field, i + 2 + dx, pl.ds(2 + dy, rows), :]

        center = c(0, 0)

        def f1(d):
            return k(0, d, 0) * c(d, 0)

        slope = (8.0 * (f1(1) - f1(-1)) - (f1(2) - f1(-2))) / 12.0

        def f2(d):
            return k(1, 0, d) * c(0, d)

        slope = slope + (8.0 * (f2(1) - f2(-1)) - (f2(2) - f2(-2))) / 12.0
        f3 = k(2, 0, 0) * center
        slope = slope + (
            8.0 * (shifted(f3, 1) - shifted(f3, -1)) - (shifted(f3, 2) - shifted(f3, -2))
        ) / 12.0
        kmid = k(3, 0, 0)
        spread = (kmid + k(3, 1, 0)) * 0.5 * (c(1, 0) - center) - (kmid + k(3, -1, 0)) * 0.5 * (
            center - c(-1, 0)
        )
        spread = (
            spread
            + (kmid + k(3, 0, 1)) * 0.5 * (c(0, 1) - center)
            - (kmid + k(3, 0, -1)) * 0.5 * (center - c(0, -1))
        )
        spread = (
            spread
            + (kmid + shifted(kmid, 1)) * 0.5 * (shifted(center, 1) - center)
            - (kmid + shifted(kmid, -1)) * 0.5 * (center - shifted(center, -1))
        )
        out_ref[0, i] = center + time_step * (scale * spread - slope)
        return carry

    lax.fori_loop(0, out_ref.shape[1], row, 0)


def stencil_step(conc_pad, coeff_pad, scale):
    count, px, py, depth = conc_pad.shape
    nx, ny = px - 4, py - 4
    return pl.pallas_call(
        stencil_body,
        out_shape=jax.ShapeDtypeStruct((count, nx, ny, depth), jnp.float32),
        grid=(count,),
        in_specs=[
            pl.BlockSpec(memory_space=pltpu.SMEM),
            pl.BlockSpec((1, px, py, depth), lambda s: (s, 0, 0, 0)),
            pl.BlockSpec(coeff_pad.shape, lambda s: (0, 0, 0, 0)),
        ],
        out_specs=pl.BlockSpec((1, nx, ny, depth), lambda s: (s, 0, 0, 0)),
        compiler_params=pltpu.CompilerParams(vmem_limit_bytes=48 * 1024 * 1024),
        cost_estimate=pl.CostEstimate(
            flops=80 * count * nx * ny * depth,
            transcendentals=0,
            bytes_accessed=4 * (conc_pad.size + coeff_pad.size + count * nx * ny * depth),
        ),
    )(scale, conc_pad, coeff_pad)


def basis_body(mix_ref, xt_ref, out_ref):
    for a in range(xt_ref.shape[0]):
        xa = xt_ref[a]
        res = jnp.dot(mix_ref[0], xa, preferred_element_type=jnp.float32)
        res = res + jnp.dot(mix_ref[1], xa, preferred_element_type=jnp.float32)
        res = res + jnp.dot(mix_ref[2], xa, preferred_element_type=jnp.float32)
        out_ref[:, a, :] = res


def basis_rows(mix_ext, static):
    hi = lax.reduce_precision(mix_ext, exponent_bits=8, mantissa_bits=7)
    rem = mix_ext - hi
    mid = lax.reduce_precision(rem, exponent_bits=8, mantissa_bits=7)
    lo = rem - mid
    parts = jnp.stack([hi, mid, lo], 0).astype(jnp.bfloat16)
    xt = jnp.transpose(static, (1, 0, 2))
    span, width, cols = xt.shape
    rows = mix_ext.shape[0]
    block = 8
    return pl.pallas_call(
        basis_body,
        out_shape=jax.ShapeDtypeStruct((rows, span, cols), jnp.float32),
        grid=(span // block,),
        in_specs=[
            pl.BlockSpec(parts.shape, lambda i: (0, 0, 0)),
            pl.BlockSpec((block, width, cols), lambda i: (i, 0, 0)),
        ],
        out_specs=pl.BlockSpec((rows, block, cols), lambda i: (0, i, 0)),
        compiler_params=pltpu.CompilerParams(vmem_limit_bytes=48 * 1024 * 1024),
        cost_estimate=pl.CostEstimate(
            flops=6 * rows * width * span * cols,
            transcendentals=0,
            bytes_accessed=2 * xt.size + 4 * rows * span * cols,
        ),
    )(parts, xt)


def per_device(scalars, velocity, diffusivity, diff_scale, basis_old, sing_values, stored):
    rank = basis_old.shape[0]
    snaps = stored.shape[0]
    static = jnp.concatenate([basis_old, stored], 0)
    weight = jnp.concatenate([sing_values, jnp.ones((snaps,), jnp.float32)], 0)
    total_rows = static.shape[1] * static.shape[2] * lax.axis_size("gx") * lax.axis_size("gy")

    local_gram = lax.dot_general(
        static, static, (((1, 2), (1, 2)), ((), ())), preferred_element_type=jnp.float32
    )
    gram_static = butterfly_sum(local_gram) * (weight[:, None] * weight[None, :]) / total_rows
    lower_static = jnp.linalg.cholesky(gram_static)
    width = rank + snaps
    inv_static = lax.linalg.triangular_solve(
        lower_static, jnp.eye(width, dtype=jnp.float32), left_side=True, lower=True
    )
    mix = inv_static * weight[None, :]
    mix_ext = jnp.concatenate([mix, jnp.zeros((1, width), jnp.float32)], 0)
    basis_ext = basis_rows(mix_ext, static)

    coeffs = jnp.concatenate([velocity, diffusivity[None]], 0)
    count = scalars.shape[0]
    first = halo(jnp.concatenate([scalars, coeffs], 0))
    coeff_pad = first[count:]
    middle0 = stencil_step(first[:1], coeff_pad, diff_scale[:1])
    result0 = stencil_step(halo(middle0), coeff_pad, diff_scale[:1])

    coarse = result0[0, ::2]
    span, depth = coarse.shape[1], coarse.shape[2]
    pick_z = (jnp.arange(depth)[:, None] == 2 * jnp.arange(depth // 2)[None, :]).astype(jnp.float32)
    pick_y = (2 * jnp.arange(span // 2)[:, None] == jnp.arange(span)[None, :]).astype(jnp.float32)
    thin = jnp.einsum("ayz,zk->ayk", coarse, pick_z, precision=lax.Precision.HIGHEST)
    fresh = jnp.einsum("jy,ayk->ajk", pick_y, thin, precision=lax.Precision.HIGHEST).reshape(
        coarse.shape[0], -1
    )
    static_f32 = static.astype(jnp.float32)
    cross = jnp.sum(static_f32 * fresh[None], axis=(1, 2))
    self_dot = jnp.sum(fresh * fresh)
    moments = butterfly_sum(jnp.concatenate([cross, self_dot[None]], 0)) / total_rows
    cross_g = moments[:width] * weight
    self_g = moments[width]

    middle_r = stencil_step(first[1:count], coeff_pad, diff_scale[1:])
    result_r = stencil_step(halo(middle_r), coeff_pad, diff_scale[1:])
    result = jnp.concatenate([result0, result_r], 0)

    link = lax.linalg.triangular_solve(
        lower_static, cross_g[:, None], left_side=True, lower=True
    )[:, 0]
    corner = jnp.sqrt(self_g - jnp.sum(link * link))
    lower = jnp.zeros((width + 1, width + 1), jnp.float32)
    lower = lower.at[:width, :width].set(lower_static)
    lower = lower.at[width, :width].set(link)
    lower = lower.at[width, width].set(corner)

    along = jnp.sum(mix * link[:, None], axis=0)
    last = (fresh - jnp.sum(static_f32 * along[:, None, None], axis=0)) / corner
    basis_new = put_last_row(basis_ext, last.reshape((1,) + basis_ext.shape[1:]))
    return (result, basis_new, lower.T)


def solution(mesh):
    return jax.shard_map(
        per_device,
        mesh=mesh,
        in_specs=(
            P(None, "gx", "gy", None),
            P(None, "gx", "gy", None),
            P("gx", "gy", None),
            P(),
            P(None, "gx", "gy"),
            P(),
            P(None, "gx", "gy"),
        ),
        out_specs=(P(None, "gx", "gy", None), P(None, "gx", "gy"), P()),
        check_vma=False,
    )
```

```python
import jax
import jax.numpy as jnp
from jax import lax
from jax.sharding import PartitionSpec as P
from jax.experimental import pallas as pl
from jax.experimental.pallas import tpu as pltpu

time_step = 0.25


def ring(axis):
    count = lax.axis_size(axis)
    forward = [(i, (i + 1) % count) for i in range(count)]
    backward = [(target, source) for source, target in forward]
    return forward, backward


def halo(block, width=2):
    fx, bx = ring("gx")
    fy, by = ring("gy")
    nx, ny = block.shape[1], block.shape[2]
    low_x = lax.ppermute(block[:, nx - width :], "gx", fx)
    high_x = lax.ppermute(block[:, :width], "gx", bx)
    low_y = lax.ppermute(block[:, :, ny - width :], "gy", fy)
    high_y = lax.ppermute(block[:, :, :width], "gy", by)
    rows = jnp.concatenate([low_x, block, high_x], axis=1)
    edge = ((0, 0), (width, width), (0, 0), (0, 0))
    return jnp.concatenate([jnp.pad(low_y, edge), rows, jnp.pad(high_y, edge)], axis=2)


def butterfly_sum(value):
    for axis in ("gx", "gy"):
        count = lax.axis_size(axis)
        bit = 1
        while bit < count:
            pairs = [(i, i ^ bit) for i in range(count)]
            value = value + lax.ppermute(value, axis, pairs)
            bit *= 2
    return value


def put_last_row(basis_ext, last):
    def body(_, last_ref, out_ref):
        out_ref[...] = last_ref[...]

    row = basis_ext.shape[0] - 1
    return pl.pallas_call(
        body,
        out_shape=jax.ShapeDtypeStruct(basis_ext.shape, basis_ext.dtype),
        grid=(1,),
        in_specs=[pl.BlockSpec(memory_space=pl.ANY), pl.BlockSpec(last.shape, lambda i: (0, 0, 0))],
        out_specs=pl.BlockSpec(last.shape, lambda i: (row, 0, 0)),
        input_output_aliases={0: 0},
    )(basis_ext, last)


def tendency(concen, coeffs, diff_scale):
    velocity = coeffs[:3]
    kappa = coeffs[3]
    center = concen[:, 2:-2, 2:-2, :]
    flux_first = velocity[0][None] * concen
    slope = (
        8.0 * (flux_first[:, 3:-1, 2:-2] - flux_first[:, 1:-3, 2:-2])
        - (flux_first[:, 4:, 2:-2] - flux_first[:, :-4, 2:-2])
    ) / 12.0
    flux_second = velocity[1][None] * concen
    slope = (
        slope
        + (
            8.0 * (flux_second[:, 2:-2, 3:-1] - flux_second[:, 2:-2, 1:-3])
            - (flux_second[:, 2:-2, 4:] - flux_second[:, 2:-2, :-4])
        )
        / 12.0
    )
    flux_third = jnp.pad(velocity[2][2:-2, 2:-2][None] * center, ((0, 0), (0, 0), (0, 0), (2, 2)))
    slope = (
        slope
        + (
            8.0 * (flux_third[..., 3:-1] - flux_third[..., 1:-3])
            - (flux_third[..., 4:] - flux_third[..., :-4])
        )
        / 12.0
    )
    kappa_mid = kappa[2:-2, 2:-2][None]
    spread = (kappa_mid + kappa[3:-1, 2:-2][None]) * 0.5 * (concen[:, 3:-1, 2:-2] - center) - (
        kappa_mid + kappa[1:-3, 2:-2][None]
    ) * 0.5 * (center - concen[:, 1:-3, 2:-2])
    spread = (
        spread
        + (kappa_mid + kappa[2:-2, 3:-1][None]) * 0.5 * (concen[:, 2:-2, 3:-1] - center)
        - (kappa_mid + kappa[2:-2, 1:-3][None]) * 0.5 * (center - concen[:, 2:-2, 1:-3])
    )
    kappa_pad = jnp.pad(kappa_mid, ((0, 0), (0, 0), (0, 0), (1, 1)))
    center_pad = jnp.pad(center, ((0, 0), (0, 0), (0, 0), (1, 1)))
    spread = (
        spread
        + (kappa_mid + kappa_pad[..., 2:]) * 0.5 * (center_pad[..., 2:] - center)
        - (kappa_mid + kappa_pad[..., :-2]) * 0.5 * (center - center_pad[..., :-2])
    )
    return center + time_step * (diff_scale[:, None, None, None] * spread - slope)


def stencil_body(scale_ref, conc_ref, coeff_ref, out_ref):
    s = pl.program_id(0)
    scale = scale_ref[s]
    rows = out_ref.shape[2]
    depth = out_ref.shape[3]
    lane = lax.broadcasted_iota(jnp.int32, (rows, depth), 1)

    def shifted(value, d):
        rolled = pltpu.roll(value, (-d) % depth, 1)
        keep = (lane + d >= 0) & (lane + d < depth)
        return jnp.where(keep, rolled, 0.0)

    def row(i, carry):
        def c(dx, dy):
            return conc_ref[0, i + 2 + dx, pl.ds(2 + dy, rows), :]

        def k(field, dx, dy):
            return coeff_ref[field, i + 2 + dx, pl.ds(2 + dy, rows), :]

        center = c(0, 0)

        def f1(d):
            return k(0, d, 0) * c(d, 0)

        slope = (8.0 * (f1(1) - f1(-1)) - (f1(2) - f1(-2))) / 12.0

        def f2(d):
            return k(1, 0, d) * c(0, d)

        slope = slope + (8.0 * (f2(1) - f2(-1)) - (f2(2) - f2(-2))) / 12.0
        f3 = k(2, 0, 0) * center
        slope = slope + (
            8.0 * (shifted(f3, 1) - shifted(f3, -1)) - (shifted(f3, 2) - shifted(f3, -2))
        ) / 12.0
        kmid = k(3, 0, 0)
        spread = (kmid + k(3, 1, 0)) * 0.5 * (c(1, 0) - center) - (kmid + k(3, -1, 0)) * 0.5 * (
            center - c(-1, 0)
        )
        spread = (
            spread
            + (kmid + k(3, 0, 1)) * 0.5 * (c(0, 1) - center)
            - (kmid + k(3, 0, -1)) * 0.5 * (center - c(0, -1))
        )
        spread = (
            spread
            + (kmid + shifted(kmid, 1)) * 0.5 * (shifted(center, 1) - center)
            - (kmid + shifted(kmid, -1)) * 0.5 * (center - shifted(center, -1))
        )
        out_ref[0, i] = center + time_step * (scale * spread - slope)
        return carry

    lax.fori_loop(0, out_ref.shape[1], row, 0)


def stencil_step(conc_pad, coeff_pad, scale):
    count, px, py, depth = conc_pad.shape
    nx, ny = px - 4, py - 4
    return pl.pallas_call(
        stencil_body,
        out_shape=jax.ShapeDtypeStruct((count, nx, ny, depth), jnp.float32),
        grid=(count,),
        in_specs=[
            pl.BlockSpec(memory_space=pltpu.SMEM),
            pl.BlockSpec((1, px, py, depth), lambda s: (s, 0, 0, 0)),
            pl.BlockSpec(coeff_pad.shape, lambda s: (0, 0, 0, 0)),
        ],
        out_specs=pl.BlockSpec((1, nx, ny, depth), lambda s: (s, 0, 0, 0)),
        compiler_params=pltpu.CompilerParams(vmem_limit_bytes=48 * 1024 * 1024),
        cost_estimate=pl.CostEstimate(
            flops=80 * count * nx * ny * depth,
            transcendentals=0,
            bytes_accessed=4 * (conc_pad.size + coeff_pad.size + count * nx * ny * depth),
        ),
    )(scale, conc_pad, coeff_pad)


def basis_body(mix_ref, xt_ref, out_ref):
    for a in range(xt_ref.shape[0]):
        xa = xt_ref[a]
        res = jnp.dot(mix_ref[0], xa, preferred_element_type=jnp.float32)
        res = res + jnp.dot(mix_ref[1], xa, preferred_element_type=jnp.float32)
        res = res + jnp.dot(mix_ref[2], xa, preferred_element_type=jnp.float32)
        out_ref[:, a, :] = res


def basis_rows(mix_ext, static):
    hi = lax.reduce_precision(mix_ext, exponent_bits=8, mantissa_bits=7)
    rem = mix_ext - hi
    mid = lax.reduce_precision(rem, exponent_bits=8, mantissa_bits=7)
    lo = rem - mid
    parts = jnp.stack([hi, mid, lo], 0).astype(jnp.bfloat16)
    xt = jnp.transpose(static, (1, 0, 2))
    span, width, cols = xt.shape
    rows = mix_ext.shape[0]
    block = 8
    return pl.pallas_call(
        basis_body,
        out_shape=jax.ShapeDtypeStruct((rows, span, cols), jnp.float32),
        grid=(span // block,),
        in_specs=[
            pl.BlockSpec(parts.shape, lambda i: (0, 0, 0)),
            pl.BlockSpec((block, width, cols), lambda i: (i, 0, 0)),
        ],
        out_specs=pl.BlockSpec((rows, block, cols), lambda i: (0, i, 0)),
        compiler_params=pltpu.CompilerParams(vmem_limit_bytes=48 * 1024 * 1024),
        cost_estimate=pl.CostEstimate(
            flops=6 * rows * width * span * cols,
            transcendentals=0,
            bytes_accessed=2 * xt.size + 4 * rows * span * cols,
        ),
    )(parts, xt)


def per_device(scalars, velocity, diffusivity, diff_scale, basis_old, sing_values, stored):
    rank = basis_old.shape[0]
    snaps = stored.shape[0]
    static = jnp.concatenate([basis_old, stored], 0)
    weight = jnp.concatenate([sing_values, jnp.ones((snaps,), jnp.float32)], 0)
    total_rows = static.shape[1] * static.shape[2] * lax.axis_size("gx") * lax.axis_size("gy")

    local_gram = lax.dot_general(
        static, static, (((1, 2), (1, 2)), ((), ())), preferred_element_type=jnp.float32
    )
    coeffs = jnp.concatenate([velocity, diffusivity[None]], 0)
    first = halo(jnp.concatenate([scalars[:1], coeffs], 0))
    coeff_pad = first[1:]
    middle0 = stencil_step(first[:1], coeff_pad, diff_scale[:1])
    local_gram, middle0 = lax.optimization_barrier((local_gram, middle0))
    gram_static = butterfly_sum(local_gram) * (weight[:, None] * weight[None, :]) / total_rows
    lower_static = jnp.linalg.cholesky(gram_static)
    width = rank + snaps
    inv_static = lax.linalg.triangular_solve(
        lower_static, jnp.eye(width, dtype=jnp.float32), left_side=True, lower=True
    )
    mix = inv_static * weight[None, :]
    mix_ext = jnp.concatenate([mix, jnp.zeros((1, width), jnp.float32)], 0)
    basis_ext = basis_rows(mix_ext, static)

    result0 = stencil_step(halo(middle0), coeff_pad, diff_scale[:1])

    coarse = result0[0, ::2]
    span, depth = coarse.shape[1], coarse.shape[2]
    pick_z = (jnp.arange(depth)[:, None] == 2 * jnp.arange(depth // 2)[None, :]).astype(jnp.float32)
    pick_y = (2 * jnp.arange(span // 2)[:, None] == jnp.arange(span)[None, :]).astype(jnp.float32)
    thin = jnp.einsum("ayz,zk->ayk", coarse, pick_z, precision=lax.Precision.HIGHEST)
    fresh = jnp.einsum("jy,ayk->ajk", pick_y, thin, precision=lax.Precision.HIGHEST).reshape(
        coarse.shape[0], -1
    )
    static_f32 = static.astype(jnp.float32)
    cross = jnp.sum(static_f32 * fresh[None], axis=(1, 2))
    self_dot = jnp.sum(fresh * fresh)
    moments = butterfly_sum(jnp.concatenate([cross, self_dot[None]], 0)) / total_rows
    cross_g = moments[:width] * weight
    self_g = moments[width]

    rest = halo(scalars[1:])
    middle_r = stencil_step(rest, coeff_pad, diff_scale[1:])
    result_r = stencil_step(halo(middle_r), coeff_pad, diff_scale[1:])
    result = jnp.concatenate([result0, result_r], 0)

    link = lax.linalg.triangular_solve(
        lower_static, cross_g[:, None], left_side=True, lower=True
    )[:, 0]
    corner = jnp.sqrt(self_g - jnp.sum(link * link))
    lower = jnp.zeros((width + 1, width + 1), jnp.float32)
    lower = lower.at[:width, :width].set(lower_static)
    lower = lower.at[width, :width].set(link)
    lower = lower.at[width, width].set(corner)

    along = jnp.sum(mix * link[:, None], axis=0)
    last = (fresh - jnp.sum(static_f32 * along[:, None, None], axis=0)) / corner
    basis_new = put_last_row(basis_ext, last.reshape((1,) + basis_ext.shape[1:]))
    return (result, basis_new, lower.T)


def solution(mesh):
    return jax.shard_map(
        per_device,
        mesh=mesh,
        in_specs=(
            P(None, "gx", "gy", None),
            P(None, "gx", "gy", None),
            P("gx", "gy", None),
            P(),
            P(None, "gx", "gy"),
            P(),
            P(None, "gx", "gy"),
        ),
        out_specs=(P(None, "gx", "gy", None), P(None, "gx", "gy"), P()),
        check_vma=False,
    )
```

```python
import jax
import jax.numpy as jnp
from jax import lax
from jax.sharding import PartitionSpec as P
from jax.experimental import pallas as pl
from jax.experimental.pallas import tpu as pltpu

time_step = 0.25


def ring(axis):
    count = lax.axis_size(axis)
    forward = [(i, (i + 1) % count) for i in range(count)]
    backward = [(target, source) for source, target in forward]
    return forward, backward


def halo(block, width=2):
    fx, bx = ring("gx")
    fy, by = ring("gy")
    nx, ny = block.shape[1], block.shape[2]
    low_x = lax.ppermute(block[:, nx - width :], "gx", fx)
    high_x = lax.ppermute(block[:, :width], "gx", bx)
    low_y = lax.ppermute(block[:, :, ny - width :], "gy", fy)
    high_y = lax.ppermute(block[:, :, :width], "gy", by)
    rows = jnp.concatenate([low_x, block, high_x], axis=1)
    edge = ((0, 0), (width, width), (0, 0), (0, 0))
    return jnp.concatenate([jnp.pad(low_y, edge), rows, jnp.pad(high_y, edge)], axis=2)


def butterfly_sum(value):
    for axis in ("gx", "gy"):
        count = lax.axis_size(axis)
        bit = 1
        while bit < count:
            pairs = [(i, i ^ bit) for i in range(count)]
            value = value + lax.ppermute(value, axis, pairs)
            bit *= 2
    return value


def put_last_row(basis_ext, last):
    def body(_, last_ref, out_ref):
        out_ref[...] = last_ref[...]

    row = basis_ext.shape[0] - 1
    return pl.pallas_call(
        body,
        out_shape=jax.ShapeDtypeStruct(basis_ext.shape, basis_ext.dtype),
        grid=(1,),
        in_specs=[pl.BlockSpec(memory_space=pl.ANY), pl.BlockSpec(last.shape, lambda i: (0, 0, 0))],
        out_specs=pl.BlockSpec(last.shape, lambda i: (row, 0, 0)),
        input_output_aliases={0: 0},
    )(basis_ext, last)


def tendency(concen, coeffs, diff_scale):
    velocity = coeffs[:3]
    kappa = coeffs[3]
    center = concen[:, 2:-2, 2:-2, :]
    flux_first = velocity[0][None] * concen
    slope = (
        8.0 * (flux_first[:, 3:-1, 2:-2] - flux_first[:, 1:-3, 2:-2])
        - (flux_first[:, 4:, 2:-2] - flux_first[:, :-4, 2:-2])
    ) / 12.0
    flux_second = velocity[1][None] * concen
    slope = (
        slope
        + (
            8.0 * (flux_second[:, 2:-2, 3:-1] - flux_second[:, 2:-2, 1:-3])
            - (flux_second[:, 2:-2, 4:] - flux_second[:, 2:-2, :-4])
        )
        / 12.0
    )
    flux_third = jnp.pad(velocity[2][2:-2, 2:-2][None] * center, ((0, 0), (0, 0), (0, 0), (2, 2)))
    slope = (
        slope
        + (
            8.0 * (flux_third[..., 3:-1] - flux_third[..., 1:-3])
            - (flux_third[..., 4:] - flux_third[..., :-4])
        )
        / 12.0
    )
    kappa_mid = kappa[2:-2, 2:-2][None]
    spread = (kappa_mid + kappa[3:-1, 2:-2][None]) * 0.5 * (concen[:, 3:-1, 2:-2] - center) - (
        kappa_mid + kappa[1:-3, 2:-2][None]
    ) * 0.5 * (center - concen[:, 1:-3, 2:-2])
    spread = (
        spread
        + (kappa_mid + kappa[2:-2, 3:-1][None]) * 0.5 * (concen[:, 2:-2, 3:-1] - center)
        - (kappa_mid + kappa[2:-2, 1:-3][None]) * 0.5 * (center - concen[:, 2:-2, 1:-3])
    )
    kappa_pad = jnp.pad(kappa_mid, ((0, 0), (0, 0), (0, 0), (1, 1)))
    center_pad = jnp.pad(center, ((0, 0), (0, 0), (0, 0), (1, 1)))
    spread = (
        spread
        + (kappa_mid + kappa_pad[..., 2:]) * 0.5 * (center_pad[..., 2:] - center)
        - (kappa_mid + kappa_pad[..., :-2]) * 0.5 * (center - center_pad[..., :-2])
    )
    return center + time_step * (diff_scale[:, None, None, None] * spread - slope)


def stencil_body(scale_ref, conc_ref, coeff_ref, out_ref):
    s = pl.program_id(0)
    scale = scale_ref[s]
    rows = out_ref.shape[2]
    depth = out_ref.shape[3]
    lane = lax.broadcasted_iota(jnp.int32, (rows, depth), 1)

    def shifted(value, d):
        rolled = pltpu.roll(value, (-d) % depth, 1)
        keep = (lane + d >= 0) & (lane + d < depth)
        return jnp.where(keep, rolled, 0.0)

    def row(i, carry):
        def c(dx, dy):
            return conc_ref[0, i + 2 + dx, pl.ds(2 + dy, rows), :]

        def k(field, dx, dy):
            return coeff_ref[field, i + 2 + dx, pl.ds(2 + dy, rows), :]

        center = c(0, 0)

        def f1(d):
            return k(0, d, 0) * c(d, 0)

        slope = (8.0 * (f1(1) - f1(-1)) - (f1(2) - f1(-2))) / 12.0

        def f2(d):
            return k(1, 0, d) * c(0, d)

        slope = slope + (8.0 * (f2(1) - f2(-1)) - (f2(2) - f2(-2))) / 12.0
        f3 = k(2, 0, 0) * center
        slope = slope + (
            8.0 * (shifted(f3, 1) - shifted(f3, -1)) - (shifted(f3, 2) - shifted(f3, -2))
        ) / 12.0
        kmid = k(3, 0, 0)
        spread = (kmid + k(3, 1, 0)) * 0.5 * (c(1, 0) - center) - (kmid + k(3, -1, 0)) * 0.5 * (
            center - c(-1, 0)
        )
        spread = (
            spread
            + (kmid + k(3, 0, 1)) * 0.5 * (c(0, 1) - center)
            - (kmid + k(3, 0, -1)) * 0.5 * (center - c(0, -1))
        )
        spread = (
            spread
            + (kmid + shifted(kmid, 1)) * 0.5 * (shifted(center, 1) - center)
            - (kmid + shifted(kmid, -1)) * 0.5 * (center - shifted(center, -1))
        )
        out_ref[0, i] = center + time_step * (scale * spread - slope)
        return carry

    lax.fori_loop(0, out_ref.shape[1], row, 0)


def stencil_step(conc_pad, coeff_pad, scale):
    count, px, py, depth = conc_pad.shape
    nx, ny = px - 4, py - 4
    return pl.pallas_call(
        stencil_body,
        out_shape=jax.ShapeDtypeStruct((count, nx, ny, depth), jnp.float32),
        grid=(count,),
        in_specs=[
            pl.BlockSpec(memory_space=pltpu.SMEM),
            pl.BlockSpec((1, px, py, depth), lambda s: (s, 0, 0, 0)),
            pl.BlockSpec(coeff_pad.shape, lambda s: (0, 0, 0, 0)),
        ],
        out_specs=pl.BlockSpec((1, nx, ny, depth), lambda s: (s, 0, 0, 0)),
        compiler_params=pltpu.CompilerParams(vmem_limit_bytes=48 * 1024 * 1024),
        cost_estimate=pl.CostEstimate(
            flops=80 * count * nx * ny * depth,
            transcendentals=0,
            bytes_accessed=4 * (conc_pad.size + coeff_pad.size + count * nx * ny * depth),
        ),
    )(scale, conc_pad, coeff_pad)


def basis_body(mix_ref, xt_ref, out_ref):
    for a in range(xt_ref.shape[0]):
        xa = xt_ref[a]
        res = jnp.dot(mix_ref[0], xa, preferred_element_type=jnp.float32)
        res = res + jnp.dot(mix_ref[1], xa, preferred_element_type=jnp.float32)
        res = res + jnp.dot(mix_ref[2], xa, preferred_element_type=jnp.float32)
        out_ref[:, a, :] = res


def basis_rows(mix_ext, static):
    hi = lax.reduce_precision(mix_ext, exponent_bits=8, mantissa_bits=7)
    rem = mix_ext - hi
    mid = lax.reduce_precision(rem, exponent_bits=8, mantissa_bits=7)
    lo = rem - mid
    parts = jnp.stack([hi, mid, lo], 0).astype(jnp.bfloat16)
    xt = jnp.transpose(static, (1, 0, 2))
    span, width, cols = xt.shape
    rows = mix_ext.shape[0]
    block = 8
    return pl.pallas_call(
        basis_body,
        out_shape=jax.ShapeDtypeStruct((rows, span, cols), jnp.float32),
        grid=(span // block,),
        in_specs=[
            pl.BlockSpec(parts.shape, lambda i: (0, 0, 0)),
            pl.BlockSpec((block, width, cols), lambda i: (i, 0, 0)),
        ],
        out_specs=pl.BlockSpec((rows, block, cols), lambda i: (0, i, 0)),
        compiler_params=pltpu.CompilerParams(vmem_limit_bytes=48 * 1024 * 1024),
        cost_estimate=pl.CostEstimate(
            flops=6 * rows * width * span * cols,
            transcendentals=0,
            bytes_accessed=2 * xt.size + 4 * rows * span * cols,
        ),
    )(parts, xt)


def per_device(scalars, velocity, diffusivity, diff_scale, basis_old, sing_values, stored):
    rank = basis_old.shape[0]
    snaps = stored.shape[0]
    static = jnp.concatenate([basis_old, stored], 0)
    weight = jnp.concatenate([sing_values, jnp.ones((snaps,), jnp.float32)], 0)
    total_rows = static.shape[1] * static.shape[2] * lax.axis_size("gx") * lax.axis_size("gy")

    local_gram = lax.dot_general(
        static, static, (((1, 2), (1, 2)), ((), ())), preferred_element_type=jnp.float32
    )
    coeffs = jnp.concatenate([velocity, diffusivity[None]], 0)
    count = scalars.shape[0]
    first = halo(jnp.concatenate([scalars, coeffs], 0))
    coeff_pad = first[count:]
    middle0 = stencil_step(first[:1], coeff_pad, diff_scale[:1])
    local_gram, middle0 = lax.optimization_barrier((local_gram, middle0))
    gram_static = butterfly_sum(local_gram) * (weight[:, None] * weight[None, :]) / total_rows
    lower_static = jnp.linalg.cholesky(gram_static)
    width = rank + snaps
    inv_static = lax.linalg.triangular_solve(
        lower_static, jnp.eye(width, dtype=jnp.float32), left_side=True, lower=True
    )
    mix = inv_static * weight[None, :]
    mix_ext = jnp.concatenate([mix, jnp.zeros((1, width), jnp.float32)], 0)
    basis_ext = basis_rows(mix_ext, static)

    result0 = stencil_step(halo(middle0), coeff_pad, diff_scale[:1])

    coarse = result0[0, ::2]
    span, depth = coarse.shape[1], coarse.shape[2]
    pick_z = (jnp.arange(depth)[:, None] == 2 * jnp.arange(depth // 2)[None, :]).astype(jnp.float32)
    pick_y = (2 * jnp.arange(span // 2)[:, None] == jnp.arange(span)[None, :]).astype(jnp.float32)
    thin = jnp.einsum("ayz,zk->ayk", coarse, pick_z, precision=lax.Precision.HIGHEST)
    fresh = jnp.einsum("jy,ayk->ajk", pick_y, thin, precision=lax.Precision.HIGHEST).reshape(
        coarse.shape[0], -1
    )
    static_f32 = static.astype(jnp.float32)
    cross = jnp.sum(static_f32 * fresh[None], axis=(1, 2))
    self_dot = jnp.sum(fresh * fresh)
    moments = butterfly_sum(jnp.concatenate([cross, self_dot[None]], 0)) / total_rows
    cross_g = moments[:width] * weight
    self_g = moments[width]

    middle_r = stencil_step(first[1:count], coeff_pad, diff_scale[1:])
    result_r = stencil_step(halo(middle_r), coeff_pad, diff_scale[1:])
    result = jnp.concatenate([result0, result_r], 0)

    link = lax.linalg.triangular_solve(
        lower_static, cross_g[:, None], left_side=True, lower=True
    )[:, 0]
    corner = jnp.sqrt(self_g - jnp.sum(link * link))
    lower = jnp.zeros((width + 1, width + 1), jnp.float32)
    lower = lower.at[:width, :width].set(lower_static)
    lower = lower.at[width, :width].set(link)
    lower = lower.at[width, width].set(corner)

    along = jnp.sum(mix * link[:, None], axis=0)
    last = (fresh - jnp.sum(static_f32 * along[:, None, None], axis=0)) / corner
    basis_new = put_last_row(basis_ext, last.reshape((1,) + basis_ext.shape[1:]))
    return (result, basis_new, lower.T)


def solution(mesh):
    return jax.shard_map(
        per_device,
        mesh=mesh,
        in_specs=(
            P(None, "gx", "gy", None),
            P(None, "gx", "gy", None),
            P("gx", "gy", None),
            P(),
            P(None, "gx", "gy"),
            P(),
            P(None, "gx", "gy"),
        ),
        out_specs=(P(None, "gx", "gy", None), P(None, "gx", "gy"), P()),
        check_vma=False,
    )
```

```python
import jax
import jax.numpy as jnp
from jax import lax
from jax.sharding import PartitionSpec as P
from jax.experimental import pallas as pl
from jax.experimental.pallas import tpu as pltpu

time_step = 0.25


def ring(axis):
    count = lax.axis_size(axis)
    forward = [(i, (i + 1) % count) for i in range(count)]
    backward = [(target, source) for source, target in forward]
    return forward, backward


def halo(block, width=2):
    fx, bx = ring("gx")
    fy, by = ring("gy")
    nx, ny = block.shape[1], block.shape[2]
    low_x = lax.ppermute(block[:, nx - width :], "gx", fx)
    high_x = lax.ppermute(block[:, :width], "gx", bx)
    low_y = lax.ppermute(block[:, :, ny - width :], "gy", fy)
    high_y = lax.ppermute(block[:, :, :width], "gy", by)
    rows = jnp.concatenate([low_x, block, high_x], axis=1)
    edge = ((0, 0), (width, width), (0, 0), (0, 0))
    return jnp.concatenate([jnp.pad(low_y, edge), rows, jnp.pad(high_y, edge)], axis=2)


def butterfly_sum(value):
    for axis in ("gx", "gy"):
        count = lax.axis_size(axis)
        bit = 1
        while bit < count:
            pairs = [(i, i ^ bit) for i in range(count)]
            value = value + lax.ppermute(value, axis, pairs)
            bit *= 2
    return value


def put_last_row(basis_ext, last):
    def body(_, last_ref, out_ref):
        out_ref[...] = last_ref[...]

    row = basis_ext.shape[0] - 1
    return pl.pallas_call(
        body,
        out_shape=jax.ShapeDtypeStruct(basis_ext.shape, basis_ext.dtype),
        grid=(1,),
        in_specs=[pl.BlockSpec(memory_space=pl.ANY), pl.BlockSpec(last.shape, lambda i: (0, 0, 0))],
        out_specs=pl.BlockSpec(last.shape, lambda i: (row, 0, 0)),
        input_output_aliases={0: 0},
    )(basis_ext, last)


def tendency(concen, coeffs, diff_scale):
    velocity = coeffs[:3]
    kappa = coeffs[3]
    center = concen[:, 2:-2, 2:-2, :]
    flux_first = velocity[0][None] * concen
    slope = (
        8.0 * (flux_first[:, 3:-1, 2:-2] - flux_first[:, 1:-3, 2:-2])
        - (flux_first[:, 4:, 2:-2] - flux_first[:, :-4, 2:-2])
    ) / 12.0
    flux_second = velocity[1][None] * concen
    slope = (
        slope
        + (
            8.0 * (flux_second[:, 2:-2, 3:-1] - flux_second[:, 2:-2, 1:-3])
            - (flux_second[:, 2:-2, 4:] - flux_second[:, 2:-2, :-4])
        )
        / 12.0
    )
    flux_third = jnp.pad(velocity[2][2:-2, 2:-2][None] * center, ((0, 0), (0, 0), (0, 0), (2, 2)))
    slope = (
        slope
        + (
            8.0 * (flux_third[..., 3:-1] - flux_third[..., 1:-3])
            - (flux_third[..., 4:] - flux_third[..., :-4])
        )
        / 12.0
    )
    kappa_mid = kappa[2:-2, 2:-2][None]
    spread = (kappa_mid + kappa[3:-1, 2:-2][None]) * 0.5 * (concen[:, 3:-1, 2:-2] - center) - (
        kappa_mid + kappa[1:-3, 2:-2][None]
    ) * 0.5 * (center - concen[:, 1:-3, 2:-2])
    spread = (
        spread
        + (kappa_mid + kappa[2:-2, 3:-1][None]) * 0.5 * (concen[:, 2:-2, 3:-1] - center)
        - (kappa_mid + kappa[2:-2, 1:-3][None]) * 0.5 * (center - concen[:, 2:-2, 1:-3])
    )
    kappa_pad = jnp.pad(kappa_mid, ((0, 0), (0, 0), (0, 0), (1, 1)))
    center_pad = jnp.pad(center, ((0, 0), (0, 0), (0, 0), (1, 1)))
    spread = (
        spread
        + (kappa_mid + kappa_pad[..., 2:]) * 0.5 * (center_pad[..., 2:] - center)
        - (kappa_mid + kappa_pad[..., :-2]) * 0.5 * (center - center_pad[..., :-2])
    )
    return center + time_step * (diff_scale[:, None, None, None] * spread - slope)


def stencil_body(scale_ref, conc_ref, coeff_ref, out_ref):
    s = pl.program_id(0)
    scale = scale_ref[s]
    rows = out_ref.shape[2]
    depth = out_ref.shape[3]
    lane = lax.broadcasted_iota(jnp.int32, (rows, depth), 1)

    def shifted(value, d):
        rolled = pltpu.roll(value, (-d) % depth, 1)
        keep = (lane + d >= 0) & (lane + d < depth)
        return jnp.where(keep, rolled, 0.0)

    def row(i, carry):
        def c(dx, dy):
            return conc_ref[0, i + 2 + dx, pl.ds(2 + dy, rows), :]

        def k(field, dx, dy):
            return coeff_ref[field, i + 2 + dx, pl.ds(2 + dy, rows), :]

        center = c(0, 0)

        def f1(d):
            return k(0, d, 0) * c(d, 0)

        slope = 8.0 * (f1(1) - f1(-1)) - (f1(2) - f1(-2))

        def f2(d):
            return k(1, 0, d) * c(0, d)

        slope = slope + (8.0 * (f2(1) - f2(-1)) - (f2(2) - f2(-2)))
        f3 = k(2, 0, 0) * center
        slope = slope + (
            8.0 * (shifted(f3, 1) - shifted(f3, -1)) - (shifted(f3, 2) - shifted(f3, -2))
        )
        slope = slope * (1.0 / 12.0)
        kmid = k(3, 0, 0)
        spread = (kmid + k(3, 1, 0)) * 0.5 * (c(1, 0) - center) - (kmid + k(3, -1, 0)) * 0.5 * (
            center - c(-1, 0)
        )
        spread = (
            spread
            + (kmid + k(3, 0, 1)) * 0.5 * (c(0, 1) - center)
            - (kmid + k(3, 0, -1)) * 0.5 * (center - c(0, -1))
        )
        spread = (
            spread
            + (kmid + shifted(kmid, 1)) * 0.5 * (shifted(center, 1) - center)
            - (kmid + shifted(kmid, -1)) * 0.5 * (center - shifted(center, -1))
        )
        out_ref[0, i] = center + time_step * (scale * spread - slope)
        return carry

    lax.fori_loop(0, out_ref.shape[1], row, 0)


def stencil_step(conc_pad, coeff_pad, scale):
    count, px, py, depth = conc_pad.shape
    nx, ny = px - 4, py - 4
    return pl.pallas_call(
        stencil_body,
        out_shape=jax.ShapeDtypeStruct((count, nx, ny, depth), jnp.float32),
        grid=(count,),
        in_specs=[
            pl.BlockSpec(memory_space=pltpu.SMEM),
            pl.BlockSpec((1, px, py, depth), lambda s: (s, 0, 0, 0)),
            pl.BlockSpec(coeff_pad.shape, lambda s: (0, 0, 0, 0)),
        ],
        out_specs=pl.BlockSpec((1, nx, ny, depth), lambda s: (s, 0, 0, 0)),
        compiler_params=pltpu.CompilerParams(vmem_limit_bytes=48 * 1024 * 1024),
        cost_estimate=pl.CostEstimate(
            flops=80 * count * nx * ny * depth,
            transcendentals=0,
            bytes_accessed=4 * (conc_pad.size + coeff_pad.size + count * nx * ny * depth),
        ),
    )(scale, conc_pad, coeff_pad)


def basis_body(mix_ref, xt_ref, out_ref):
    for a in range(xt_ref.shape[0]):
        xa = xt_ref[a]
        res = jnp.dot(mix_ref[0], xa, preferred_element_type=jnp.float32)
        res = res + jnp.dot(mix_ref[1], xa, preferred_element_type=jnp.float32)
        res = res + jnp.dot(mix_ref[2], xa, preferred_element_type=jnp.float32)
        out_ref[:, a, :] = res


def basis_rows(mix_ext, static):
    hi = lax.reduce_precision(mix_ext, exponent_bits=8, mantissa_bits=7)
    rem = mix_ext - hi
    mid = lax.reduce_precision(rem, exponent_bits=8, mantissa_bits=7)
    lo = rem - mid
    parts = jnp.stack([hi, mid, lo], 0).astype(jnp.bfloat16)
    xt = jnp.transpose(static, (1, 0, 2))
    span, width, cols = xt.shape
    rows = mix_ext.shape[0]
    block = 8
    return pl.pallas_call(
        basis_body,
        out_shape=jax.ShapeDtypeStruct((rows, span, cols), jnp.float32),
        grid=(span // block,),
        in_specs=[
            pl.BlockSpec(parts.shape, lambda i: (0, 0, 0)),
            pl.BlockSpec((block, width, cols), lambda i: (i, 0, 0)),
        ],
        out_specs=pl.BlockSpec((rows, block, cols), lambda i: (0, i, 0)),
        compiler_params=pltpu.CompilerParams(vmem_limit_bytes=48 * 1024 * 1024),
        cost_estimate=pl.CostEstimate(
            flops=6 * rows * width * span * cols,
            transcendentals=0,
            bytes_accessed=2 * xt.size + 4 * rows * span * cols,
        ),
    )(parts, xt)


def per_device(scalars, velocity, diffusivity, diff_scale, basis_old, sing_values, stored):
    rank = basis_old.shape[0]
    snaps = stored.shape[0]
    static = jnp.concatenate([basis_old, stored], 0)
    weight = jnp.concatenate([sing_values, jnp.ones((snaps,), jnp.float32)], 0)
    total_rows = static.shape[1] * static.shape[2] * lax.axis_size("gx") * lax.axis_size("gy")

    local_gram = lax.dot_general(
        static, static, (((1, 2), (1, 2)), ((), ())), preferred_element_type=jnp.float32
    )
    coeffs = jnp.concatenate([velocity, diffusivity[None]], 0)
    count = scalars.shape[0]
    first = halo(jnp.concatenate([scalars, coeffs], 0))
    coeff_pad = first[count:]
    middle0 = stencil_step(first[:1], coeff_pad, diff_scale[:1])
    local_gram, middle0 = lax.optimization_barrier((local_gram, middle0))
    gram_static = butterfly_sum(local_gram) * (weight[:, None] * weight[None, :]) / total_rows
    lower_static = jnp.linalg.cholesky(gram_static)
    width = rank + snaps
    inv_static = lax.linalg.triangular_solve(
        lower_static, jnp.eye(width, dtype=jnp.float32), left_side=True, lower=True
    )
    mix = inv_static * weight[None, :]
    mix_ext = jnp.concatenate([mix, jnp.zeros((1, width), jnp.float32)], 0)
    basis_ext = basis_rows(mix_ext, static)

    result0 = stencil_step(halo(middle0), coeff_pad, diff_scale[:1])

    coarse = result0[0, ::2]
    span, depth = coarse.shape[1], coarse.shape[2]
    pick_z = (jnp.arange(depth)[:, None] == 2 * jnp.arange(depth // 2)[None, :]).astype(jnp.float32)
    pick_y = (2 * jnp.arange(span // 2)[:, None] == jnp.arange(span)[None, :]).astype(jnp.float32)
    thin = jnp.einsum("ayz,zk->ayk", coarse, pick_z, precision=lax.Precision.HIGHEST)
    fresh = jnp.einsum("jy,ayk->ajk", pick_y, thin, precision=lax.Precision.HIGHEST).reshape(
        coarse.shape[0], -1
    )
    static_f32 = static.astype(jnp.float32)
    cross = jnp.sum(static_f32 * fresh[None], axis=(1, 2))
    self_dot = jnp.sum(fresh * fresh)
    moments = butterfly_sum(jnp.concatenate([cross, self_dot[None]], 0)) / total_rows
    cross_g = moments[:width] * weight
    self_g = moments[width]

    middle_r = stencil_step(first[1:count], coeff_pad, diff_scale[1:])
    result_r = stencil_step(halo(middle_r), coeff_pad, diff_scale[1:])
    result = jnp.concatenate([result0, result_r], 0)

    link = lax.linalg.triangular_solve(
        lower_static, cross_g[:, None], left_side=True, lower=True
    )[:, 0]
    corner = jnp.sqrt(self_g - jnp.sum(link * link))
    lower = jnp.zeros((width + 1, width + 1), jnp.float32)
    lower = lower.at[:width, :width].set(lower_static)
    lower = lower.at[width, :width].set(link)
    lower = lower.at[width, width].set(corner)

    along = jnp.sum(mix * link[:, None], axis=0)
    last = (fresh - jnp.sum(static_f32 * along[:, None, None], axis=0)) / corner
    basis_new = put_last_row(basis_ext, last.reshape((1,) + basis_ext.shape[1:]))
    return (result, basis_new, lower.T)


def solution(mesh):
    return jax.shard_map(
        per_device,
        mesh=mesh,
        in_specs=(
            P(None, "gx", "gy", None),
            P(None, "gx", "gy", None),
            P("gx", "gy", None),
            P(),
            P(None, "gx", "gy"),
            P(),
            P(None, "gx", "gy"),
        ),
        out_specs=(P(None, "gx", "gy", None), P(None, "gx", "gy"), P()),
        check_vma=False,
    )
```

```python
import jax
import jax.numpy as jnp
from jax import lax
from jax.sharding import PartitionSpec as P
from jax.experimental import pallas as pl
from jax.experimental.pallas import tpu as pltpu

time_step = 0.25
ALIGN = 8


def ring(axis):
    count = lax.axis_size(axis)
    forward = [(i, (i + 1) % count) for i in range(count)]
    backward = [(target, source) for source, target in forward]
    return forward, backward


def halo(block, width=2):
    fx, bx = ring("gx")
    fy, by = ring("gy")
    nx, ny = block.shape[1], block.shape[2]
    low_x = lax.ppermute(block[:, nx - width :], "gx", fx)
    high_x = lax.ppermute(block[:, :width], "gx", bx)
    low_y = lax.ppermute(block[:, :, ny - width :], "gy", fy)
    high_y = lax.ppermute(block[:, :, :width], "gy", by)
    rows = jnp.concatenate([low_x, block, high_x], axis=1)
    edge = ((0, 0), (width, width), (0, 0), (0, 0))
    gap = jnp.zeros(rows.shape[:2] + (ALIGN - width,) + rows.shape[3:], rows.dtype)
    return jnp.concatenate(
        [gap, jnp.pad(low_y, edge), rows, jnp.pad(high_y, edge), gap], axis=2
    )


def butterfly_sum(value):
    for axis in ("gx", "gy"):
        count = lax.axis_size(axis)
        bit = 1
        while bit < count:
            pairs = [(i, i ^ bit) for i in range(count)]
            value = value + lax.ppermute(value, axis, pairs)
            bit *= 2
    return value


def put_last_row(basis_ext, last):
    def body(_, last_ref, out_ref):
        out_ref[...] = last_ref[...]

    row = basis_ext.shape[0] - 1
    return pl.pallas_call(
        body,
        out_shape=jax.ShapeDtypeStruct(basis_ext.shape, basis_ext.dtype),
        grid=(1,),
        in_specs=[pl.BlockSpec(memory_space=pl.ANY), pl.BlockSpec(last.shape, lambda i: (0, 0, 0))],
        out_specs=pl.BlockSpec(last.shape, lambda i: (row, 0, 0)),
        input_output_aliases={0: 0},
    )(basis_ext, last)


def tendency(concen, coeffs, diff_scale):
    velocity = coeffs[:3]
    kappa = coeffs[3]
    center = concen[:, 2:-2, 2:-2, :]
    flux_first = velocity[0][None] * concen
    slope = (
        8.0 * (flux_first[:, 3:-1, 2:-2] - flux_first[:, 1:-3, 2:-2])
        - (flux_first[:, 4:, 2:-2] - flux_first[:, :-4, 2:-2])
    ) / 12.0
    flux_second = velocity[1][None] * concen
    slope = (
        slope
        + (
            8.0 * (flux_second[:, 2:-2, 3:-1] - flux_second[:, 2:-2, 1:-3])
            - (flux_second[:, 2:-2, 4:] - flux_second[:, 2:-2, :-4])
        )
        / 12.0
    )
    flux_third = jnp.pad(velocity[2][2:-2, 2:-2][None] * center, ((0, 0), (0, 0), (0, 0), (2, 2)))
    slope = (
        slope
        + (
            8.0 * (flux_third[..., 3:-1] - flux_third[..., 1:-3])
            - (flux_third[..., 4:] - flux_third[..., :-4])
        )
        / 12.0
    )
    kappa_mid = kappa[2:-2, 2:-2][None]
    spread = (kappa_mid + kappa[3:-1, 2:-2][None]) * 0.5 * (concen[:, 3:-1, 2:-2] - center) - (
        kappa_mid + kappa[1:-3, 2:-2][None]
    ) * 0.5 * (center - concen[:, 1:-3, 2:-2])
    spread = (
        spread
        + (kappa_mid + kappa[2:-2, 3:-1][None]) * 0.5 * (concen[:, 2:-2, 3:-1] - center)
        - (kappa_mid + kappa[2:-2, 1:-3][None]) * 0.5 * (center - concen[:, 2:-2, 1:-3])
    )
    kappa_pad = jnp.pad(kappa_mid, ((0, 0), (0, 0), (0, 0), (1, 1)))
    center_pad = jnp.pad(center, ((0, 0), (0, 0), (0, 0), (1, 1)))
    spread = (
        spread
        + (kappa_mid + kappa_pad[..., 2:]) * 0.5 * (center_pad[..., 2:] - center)
        - (kappa_mid + kappa_pad[..., :-2]) * 0.5 * (center - center_pad[..., :-2])
    )
    return center + time_step * (diff_scale[:, None, None, None] * spread - slope)


def stencil_body(scale_ref, conc_ref, coeff_ref, out_ref):
    s = pl.program_id(0)
    scale = scale_ref[s]
    rows = out_ref.shape[2]
    depth = out_ref.shape[3]
    lane = lax.broadcasted_iota(jnp.int32, (rows, depth), 1)

    def shifted(value, d):
        rolled = pltpu.roll(value, (-d) % depth, 1)
        keep = (lane + d >= 0) & (lane + d < depth)
        return jnp.where(keep, rolled, 0.0)

    def row(i, carry):
        def c(dx, dy):
            return conc_ref[0, i + 2 + dx, pl.ds(ALIGN + dy, rows), :]

        def k(field, dx, dy):
            return coeff_ref[field, i + 2 + dx, pl.ds(ALIGN + dy, rows), :]

        center = c(0, 0)

        def f1(d):
            return k(0, d, 0) * c(d, 0)

        slope = 8.0 * (f1(1) - f1(-1)) - (f1(2) - f1(-2))

        def f2(d):
            return k(1, 0, d) * c(0, d)

        slope = slope + (8.0 * (f2(1) - f2(-1)) - (f2(2) - f2(-2)))
        f3 = k(2, 0, 0) * center
        slope = slope + (
            8.0 * (shifted(f3, 1) - shifted(f3, -1)) - (shifted(f3, 2) - shifted(f3, -2))
        )
        slope = slope * (1.0 / 12.0)
        kmid = k(3, 0, 0)
        spread = (kmid + k(3, 1, 0)) * 0.5 * (c(1, 0) - center) - (kmid + k(3, -1, 0)) * 0.5 * (
            center - c(-1, 0)
        )
        spread = (
            spread
            + (kmid + k(3, 0, 1)) * 0.5 * (c(0, 1) - center)
            - (kmid + k(3, 0, -1)) * 0.5 * (center - c(0, -1))
        )
        spread = (
            spread
            + (kmid + shifted(kmid, 1)) * 0.5 * (shifted(center, 1) - center)
            - (kmid + shifted(kmid, -1)) * 0.5 * (center - shifted(center, -1))
        )
        out_ref[0, i] = center + time_step * (scale * spread - slope)
        return carry

    lax.fori_loop(0, out_ref.shape[1], row, 0)


def stencil_step(conc_pad, coeff_pad, scale):
    count, px, py, depth = conc_pad.shape
    nx, ny = px - 4, py - 2 * ALIGN
    return pl.pallas_call(
        stencil_body,
        out_shape=jax.ShapeDtypeStruct((count, nx, ny, depth), jnp.float32),
        grid=(count,),
        in_specs=[
            pl.BlockSpec(memory_space=pltpu.SMEM),
            pl.BlockSpec((1, px, py, depth), lambda s: (s, 0, 0, 0)),
            pl.BlockSpec(coeff_pad.shape, lambda s: (0, 0, 0, 0)),
        ],
        out_specs=pl.BlockSpec((1, nx, ny, depth), lambda s: (s, 0, 0, 0)),
        compiler_params=pltpu.CompilerParams(vmem_limit_bytes=48 * 1024 * 1024),
        cost_estimate=pl.CostEstimate(
            flops=80 * count * nx * ny * depth,
            transcendentals=0,
            bytes_accessed=4 * (conc_pad.size + coeff_pad.size + count * nx * ny * depth),
        ),
    )(scale, conc_pad, coeff_pad)


def basis_body(mix_ref, xt_ref, out_ref):
    for a in range(xt_ref.shape[0]):
        xa = xt_ref[a]
        res = jnp.dot(mix_ref[0], xa, preferred_element_type=jnp.float32)
        res = res + jnp.dot(mix_ref[1], xa, preferred_element_type=jnp.float32)
        res = res + jnp.dot(mix_ref[2], xa, preferred_element_type=jnp.float32)
        out_ref[:, a, :] = res


def basis_rows(mix_ext, static):
    hi = lax.reduce_precision(mix_ext, exponent_bits=8, mantissa_bits=7)
    rem = mix_ext - hi
    mid = lax.reduce_precision(rem, exponent_bits=8, mantissa_bits=7)
    lo = rem - mid
    parts = jnp.stack([hi, mid, lo], 0).astype(jnp.bfloat16)
    xt = jnp.transpose(static, (1, 0, 2))
    span, width, cols = xt.shape
    rows = mix_ext.shape[0]
    block = 8
    return pl.pallas_call(
        basis_body,
        out_shape=jax.ShapeDtypeStruct((rows, span, cols), jnp.float32),
        grid=(span // block,),
        in_specs=[
            pl.BlockSpec(parts.shape, lambda i: (0, 0, 0)),
            pl.BlockSpec((block, width, cols), lambda i: (i, 0, 0)),
        ],
        out_specs=pl.BlockSpec((rows, block, cols), lambda i: (0, i, 0)),
        compiler_params=pltpu.CompilerParams(vmem_limit_bytes=48 * 1024 * 1024),
        cost_estimate=pl.CostEstimate(
            flops=6 * rows * width * span * cols,
            transcendentals=0,
            bytes_accessed=2 * xt.size + 4 * rows * span * cols,
        ),
    )(parts, xt)


def per_device(scalars, velocity, diffusivity, diff_scale, basis_old, sing_values, stored):
    rank = basis_old.shape[0]
    snaps = stored.shape[0]
    static = jnp.concatenate([basis_old, stored], 0)
    weight = jnp.concatenate([sing_values, jnp.ones((snaps,), jnp.float32)], 0)
    total_rows = static.shape[1] * static.shape[2] * lax.axis_size("gx") * lax.axis_size("gy")

    local_gram = lax.dot_general(
        static, static, (((1, 2), (1, 2)), ((), ())), preferred_element_type=jnp.float32
    )
    coeffs = jnp.concatenate([velocity, diffusivity[None]], 0)
    count = scalars.shape[0]
    first = halo(jnp.concatenate([scalars, coeffs], 0))
    coeff_pad = first[count:]
    middle0 = stencil_step(first[:1], coeff_pad, diff_scale[:1])
    local_gram, middle0 = lax.optimization_barrier((local_gram, middle0))
    gram_static = butterfly_sum(local_gram) * (weight[:, None] * weight[None, :]) / total_rows
    lower_static = jnp.linalg.cholesky(gram_static)
    width = rank + snaps
    inv_static = lax.linalg.triangular_solve(
        lower_static, jnp.eye(width, dtype=jnp.float32), left_side=True, lower=True
    )
    mix = inv_static * weight[None, :]
    mix_ext = jnp.concatenate([mix, jnp.zeros((1, width), jnp.float32)], 0)
    basis_ext = basis_rows(mix_ext, static)

    result0 = stencil_step(halo(middle0), coeff_pad, diff_scale[:1])

    coarse = result0[0, ::2]
    span, depth = coarse.shape[1], coarse.shape[2]
    pick_z = (jnp.arange(depth)[:, None] == 2 * jnp.arange(depth // 2)[None, :]).astype(jnp.float32)
    pick_y = (2 * jnp.arange(span // 2)[:, None] == jnp.arange(span)[None, :]).astype(jnp.float32)
    thin = jnp.einsum("ayz,zk->ayk", coarse, pick_z, precision=lax.Precision.HIGHEST)
    fresh = jnp.einsum("jy,ayk->ajk", pick_y, thin, precision=lax.Precision.HIGHEST).reshape(
        coarse.shape[0], -1
    )
    static_f32 = static.astype(jnp.float32)
    cross = jnp.sum(static_f32 * fresh[None], axis=(1, 2))
    self_dot = jnp.sum(fresh * fresh)
    moments = butterfly_sum(jnp.concatenate([cross, self_dot[None]], 0)) / total_rows
    cross_g = moments[:width] * weight
    self_g = moments[width]

    middle_r = stencil_step(first[1:count], coeff_pad, diff_scale[1:])
    result_r = stencil_step(halo(middle_r), coeff_pad, diff_scale[1:])
    result = jnp.concatenate([result0, result_r], 0)

    link = lax.linalg.triangular_solve(
        lower_static, cross_g[:, None], left_side=True, lower=True
    )[:, 0]
    corner = jnp.sqrt(self_g - jnp.sum(link * link))
    lower = jnp.zeros((width + 1, width + 1), jnp.float32)
    lower = lower.at[:width, :width].set(lower_static)
    lower = lower.at[width, :width].set(link)
    lower = lower.at[width, width].set(corner)

    along = jnp.sum(mix * link[:, None], axis=0)
    last = (fresh - jnp.sum(static_f32 * along[:, None, None], axis=0)) / corner
    basis_new = put_last_row(basis_ext, last.reshape((1,) + basis_ext.shape[1:]))
    return (result, basis_new, lower.T)


def solution(mesh):
    return jax.shard_map(
        per_device,
        mesh=mesh,
        in_specs=(
            P(None, "gx", "gy", None),
            P(None, "gx", "gy", None),
            P("gx", "gy", None),
            P(),
            P(None, "gx", "gy"),
            P(),
            P(None, "gx", "gy"),
        ),
        out_specs=(P(None, "gx", "gy", None), P(None, "gx", "gy"), P()),
        check_vma=False,
    )
```

```python
import jax
import jax.numpy as jnp
from jax import lax
from jax.sharding import PartitionSpec as P
from jax.experimental import pallas as pl
from jax.experimental.pallas import tpu as pltpu

time_step = 0.25


def ring(axis):
    count = lax.axis_size(axis)
    forward = [(i, (i + 1) % count) for i in range(count)]
    backward = [(target, source) for source, target in forward]
    return forward, backward


def halo(block, width=2):
    fx, bx = ring("gx")
    fy, by = ring("gy")
    nx, ny = block.shape[1], block.shape[2]
    low_x = lax.ppermute(block[:, nx - width :], "gx", fx)
    high_x = lax.ppermute(block[:, :width], "gx", bx)
    low_y = lax.ppermute(block[:, :, ny - width :], "gy", fy)
    high_y = lax.ppermute(block[:, :, :width], "gy", by)
    rows = jnp.concatenate([low_x, block, high_x], axis=1)
    edge = ((0, 0), (width, width), (0, 0), (0, 0))
    return jnp.concatenate([jnp.pad(low_y, edge), rows, jnp.pad(high_y, edge)], axis=2)


def butterfly_sum(value):
    for axis in ("gx", "gy"):
        count = lax.axis_size(axis)
        bit = 1
        while bit < count:
            pairs = [(i, i ^ bit) for i in range(count)]
            value = value + lax.ppermute(value, axis, pairs)
            bit *= 2
    return value


def put_last_row(basis_ext, last):
    def body(_, last_ref, out_ref):
        out_ref[...] = last_ref[...]

    row = basis_ext.shape[0] - 1
    return pl.pallas_call(
        body,
        out_shape=jax.ShapeDtypeStruct(basis_ext.shape, basis_ext.dtype),
        grid=(1,),
        in_specs=[pl.BlockSpec(memory_space=pl.ANY), pl.BlockSpec(last.shape, lambda i: (0, 0, 0))],
        out_specs=pl.BlockSpec(last.shape, lambda i: (row, 0, 0)),
        input_output_aliases={0: 0},
    )(basis_ext, last)


def tendency(concen, coeffs, diff_scale):
    velocity = coeffs[:3]
    kappa = coeffs[3]
    center = concen[:, 2:-2, 2:-2, :]
    flux_first = velocity[0][None] * concen
    slope = (
        8.0 * (flux_first[:, 3:-1, 2:-2] - flux_first[:, 1:-3, 2:-2])
        - (flux_first[:, 4:, 2:-2] - flux_first[:, :-4, 2:-2])
    ) / 12.0
    flux_second = velocity[1][None] * concen
    slope = (
        slope
        + (
            8.0 * (flux_second[:, 2:-2, 3:-1] - flux_second[:, 2:-2, 1:-3])
            - (flux_second[:, 2:-2, 4:] - flux_second[:, 2:-2, :-4])
        )
        / 12.0
    )
    flux_third = jnp.pad(velocity[2][2:-2, 2:-2][None] * center, ((0, 0), (0, 0), (0, 0), (2, 2)))
    slope = (
        slope
        + (
            8.0 * (flux_third[..., 3:-1] - flux_third[..., 1:-3])
            - (flux_third[..., 4:] - flux_third[..., :-4])
        )
        / 12.0
    )
    kappa_mid = kappa[2:-2, 2:-2][None]
    spread = (kappa_mid + kappa[3:-1, 2:-2][None]) * 0.5 * (concen[:, 3:-1, 2:-2] - center) - (
        kappa_mid + kappa[1:-3, 2:-2][None]
    ) * 0.5 * (center - concen[:, 1:-3, 2:-2])
    spread = (
        spread
        + (kappa_mid + kappa[2:-2, 3:-1][None]) * 0.5 * (concen[:, 2:-2, 3:-1] - center)
        - (kappa_mid + kappa[2:-2, 1:-3][None]) * 0.5 * (center - concen[:, 2:-2, 1:-3])
    )
    kappa_pad = jnp.pad(kappa_mid, ((0, 0), (0, 0), (0, 0), (1, 1)))
    center_pad = jnp.pad(center, ((0, 0), (0, 0), (0, 0), (1, 1)))
    spread = (
        spread
        + (kappa_mid + kappa_pad[..., 2:]) * 0.5 * (center_pad[..., 2:] - center)
        - (kappa_mid + kappa_pad[..., :-2]) * 0.5 * (center - center_pad[..., :-2])
    )
    return center + time_step * (diff_scale[:, None, None, None] * spread - slope)


def stencil_body(scale_ref, conc_ref, coeff_ref, out_ref):
    s = pl.program_id(0)
    scale = scale_ref[s]
    rows = out_ref.shape[2]
    depth = out_ref.shape[3]
    lane = lax.broadcasted_iota(jnp.int32, (rows, depth), 1)

    def shifted(value, d):
        rolled = pltpu.roll(value, (-d) % depth, 1)
        keep = (lane + d >= 0) & (lane + d < depth)
        return jnp.where(keep, rolled, 0.0)

    def row(i, carry):
        def c(dx, dy):
            return conc_ref[0, i + 2 + dx, pl.ds(2 + dy, rows), :]

        def k(field, dx, dy):
            return coeff_ref[field, i + 2 + dx, pl.ds(2 + dy, rows), :]

        center = c(0, 0)

        def f1(d):
            return k(0, d, 0) * c(d, 0)

        slope = 8.0 * (f1(1) - f1(-1)) - (f1(2) - f1(-2))

        def f2(d):
            return k(1, 0, d) * c(0, d)

        slope = slope + (8.0 * (f2(1) - f2(-1)) - (f2(2) - f2(-2)))
        f3 = k(2, 0, 0) * center
        slope = slope + (
            8.0 * (shifted(f3, 1) - shifted(f3, -1)) - (shifted(f3, 2) - shifted(f3, -2))
        )
        slope = slope * (1.0 / 12.0)
        kmid = k(3, 0, 0)
        spread = (kmid + k(3, 1, 0)) * 0.5 * (c(1, 0) - center) - (kmid + k(3, -1, 0)) * 0.5 * (
            center - c(-1, 0)
        )
        spread = (
            spread
            + (kmid + k(3, 0, 1)) * 0.5 * (c(0, 1) - center)
            - (kmid + k(3, 0, -1)) * 0.5 * (center - c(0, -1))
        )
        spread = (
            spread
            + (kmid + shifted(kmid, 1)) * 0.5 * (shifted(center, 1) - center)
            - (kmid + shifted(kmid, -1)) * 0.5 * (center - shifted(center, -1))
        )
        out_ref[0, i] = center + time_step * (scale * spread - slope)
        return carry

    lax.fori_loop(0, out_ref.shape[1], row, 0, unroll=4)


def stencil_step(conc_pad, coeff_pad, scale):
    count, px, py, depth = conc_pad.shape
    nx, ny = px - 4, py - 4
    return pl.pallas_call(
        stencil_body,
        out_shape=jax.ShapeDtypeStruct((count, nx, ny, depth), jnp.float32),
        grid=(count,),
        in_specs=[
            pl.BlockSpec(memory_space=pltpu.SMEM),
            pl.BlockSpec((1, px, py, depth), lambda s: (s, 0, 0, 0)),
            pl.BlockSpec(coeff_pad.shape, lambda s: (0, 0, 0, 0)),
        ],
        out_specs=pl.BlockSpec((1, nx, ny, depth), lambda s: (s, 0, 0, 0)),
        compiler_params=pltpu.CompilerParams(vmem_limit_bytes=48 * 1024 * 1024),
        cost_estimate=pl.CostEstimate(
            flops=80 * count * nx * ny * depth,
            transcendentals=0,
            bytes_accessed=4 * (conc_pad.size + coeff_pad.size + count * nx * ny * depth),
        ),
    )(scale, conc_pad, coeff_pad)


def basis_body(mix_ref, xt_ref, out_ref):
    for a in range(xt_ref.shape[0]):
        xa = xt_ref[a]
        res = jnp.dot(mix_ref[0], xa, preferred_element_type=jnp.float32)
        res = res + jnp.dot(mix_ref[1], xa, preferred_element_type=jnp.float32)
        res = res + jnp.dot(mix_ref[2], xa, preferred_element_type=jnp.float32)
        out_ref[:, a, :] = res


def basis_rows(mix_ext, static):
    hi = lax.reduce_precision(mix_ext, exponent_bits=8, mantissa_bits=7)
    rem = mix_ext - hi
    mid = lax.reduce_precision(rem, exponent_bits=8, mantissa_bits=7)
    lo = rem - mid
    parts = jnp.stack([hi, mid, lo], 0).astype(jnp.bfloat16)
    xt = jnp.transpose(static, (1, 0, 2))
    span, width, cols = xt.shape
    rows = mix_ext.shape[0]
    block = 8
    return pl.pallas_call(
        basis_body,
        out_shape=jax.ShapeDtypeStruct((rows, span, cols), jnp.float32),
        grid=(span // block,),
        in_specs=[
            pl.BlockSpec(parts.shape, lambda i: (0, 0, 0)),
            pl.BlockSpec((block, width, cols), lambda i: (i, 0, 0)),
        ],
        out_specs=pl.BlockSpec((rows, block, cols), lambda i: (0, i, 0)),
        compiler_params=pltpu.CompilerParams(vmem_limit_bytes=48 * 1024 * 1024),
        cost_estimate=pl.CostEstimate(
            flops=6 * rows * width * span * cols,
            transcendentals=0,
            bytes_accessed=2 * xt.size + 4 * rows * span * cols,
        ),
    )(parts, xt)


def per_device(scalars, velocity, diffusivity, diff_scale, basis_old, sing_values, stored):
    rank = basis_old.shape[0]
    snaps = stored.shape[0]
    static = jnp.concatenate([basis_old, stored], 0)
    weight = jnp.concatenate([sing_values, jnp.ones((snaps,), jnp.float32)], 0)
    total_rows = static.shape[1] * static.shape[2] * lax.axis_size("gx") * lax.axis_size("gy")

    local_gram = lax.dot_general(
        static, static, (((1, 2), (1, 2)), ((), ())), preferred_element_type=jnp.float32
    )
    coeffs = jnp.concatenate([velocity, diffusivity[None]], 0)
    count = scalars.shape[0]
    first = halo(jnp.concatenate([scalars, coeffs], 0))
    coeff_pad = first[count:]
    middle0 = stencil_step(first[:1], coeff_pad, diff_scale[:1])
    local_gram, middle0 = lax.optimization_barrier((local_gram, middle0))
    gram_static = butterfly_sum(local_gram) * (weight[:, None] * weight[None, :]) / total_rows
    lower_static = jnp.linalg.cholesky(gram_static)
    width = rank + snaps
    inv_static = lax.linalg.triangular_solve(
        lower_static, jnp.eye(width, dtype=jnp.float32), left_side=True, lower=True
    )
    mix = inv_static * weight[None, :]
    mix_ext = jnp.concatenate([mix, jnp.zeros((1, width), jnp.float32)], 0)
    basis_ext = basis_rows(mix_ext, static)

    result0 = stencil_step(halo(middle0), coeff_pad, diff_scale[:1])

    coarse = result0[0, ::2]
    span, depth = coarse.shape[1], coarse.shape[2]
    pick_z = (jnp.arange(depth)[:, None] == 2 * jnp.arange(depth // 2)[None, :]).astype(jnp.float32)
    pick_y = (2 * jnp.arange(span // 2)[:, None] == jnp.arange(span)[None, :]).astype(jnp.float32)
    thin = jnp.einsum("ayz,zk->ayk", coarse, pick_z, precision=lax.Precision.HIGHEST)
    fresh = jnp.einsum("jy,ayk->ajk", pick_y, thin, precision=lax.Precision.HIGHEST).reshape(
        coarse.shape[0], -1
    )
    static_f32 = static.astype(jnp.float32)
    cross = jnp.sum(static_f32 * fresh[None], axis=(1, 2))
    self_dot = jnp.sum(fresh * fresh)
    moments = butterfly_sum(jnp.concatenate([cross, self_dot[None]], 0)) / total_rows
    cross_g = moments[:width] * weight
    self_g = moments[width]

    middle_r = stencil_step(first[1:count], coeff_pad, diff_scale[1:])
    result_r = stencil_step(halo(middle_r), coeff_pad, diff_scale[1:])
    result = jnp.concatenate([result0, result_r], 0)

    link = lax.linalg.triangular_solve(
        lower_static, cross_g[:, None], left_side=True, lower=True
    )[:, 0]
    corner = jnp.sqrt(self_g - jnp.sum(link * link))
    lower = jnp.zeros((width + 1, width + 1), jnp.float32)
    lower = lower.at[:width, :width].set(lower_static)
    lower = lower.at[width, :width].set(link)
    lower = lower.at[width, width].set(corner)

    along = jnp.sum(mix * link[:, None], axis=0)
    last = (fresh - jnp.sum(static_f32 * along[:, None, None], axis=0)) / corner
    basis_new = put_last_row(basis_ext, last.reshape((1,) + basis_ext.shape[1:]))
    return (result, basis_new, lower.T)


def solution(mesh):
    return jax.shard_map(
        per_device,
        mesh=mesh,
        in_specs=(
            P(None, "gx", "gy", None),
            P(None, "gx", "gy", None),
            P("gx", "gy", None),
            P(),
            P(None, "gx", "gy"),
            P(),
            P(None, "gx", "gy"),
        ),
        out_specs=(P(None, "gx", "gy", None), P(None, "gx", "gy"), P()),
        check_vma=False,
    )
```

```python
import jax
import jax.numpy as jnp
from jax import lax
from jax.sharding import PartitionSpec as P
from jax.experimental import pallas as pl
from jax.experimental.pallas import tpu as pltpu

time_step = 0.25


def ring(axis):
    count = lax.axis_size(axis)
    forward = [(i, (i + 1) % count) for i in range(count)]
    backward = [(target, source) for source, target in forward]
    return forward, backward


def halo(block, width=2):
    fx, bx = ring("gx")
    fy, by = ring("gy")
    nx, ny = block.shape[1], block.shape[2]
    low_x = lax.ppermute(block[:, nx - width :], "gx", fx)
    high_x = lax.ppermute(block[:, :width], "gx", bx)
    low_y = lax.ppermute(block[:, :, ny - width :], "gy", fy)
    high_y = lax.ppermute(block[:, :, :width], "gy", by)
    rows = jnp.concatenate([low_x, block, high_x], axis=1)
    edge = ((0, 0), (width, width), (0, 0), (0, 0))
    return jnp.concatenate([jnp.pad(low_y, edge), rows, jnp.pad(high_y, edge)], axis=2)


def butterfly_sum(value):
    for axis in ("gx", "gy"):
        count = lax.axis_size(axis)
        bit = 1
        while bit < count:
            pairs = [(i, i ^ bit) for i in range(count)]
            value = value + lax.ppermute(value, axis, pairs)
            bit *= 2
    return value


def put_last_row(basis_ext, last):
    def body(_, last_ref, out_ref):
        out_ref[...] = last_ref[...]

    row = basis_ext.shape[0] - 1
    return pl.pallas_call(
        body,
        out_shape=jax.ShapeDtypeStruct(basis_ext.shape, basis_ext.dtype),
        grid=(1,),
        in_specs=[pl.BlockSpec(memory_space=pl.ANY), pl.BlockSpec(last.shape, lambda i: (0, 0, 0))],
        out_specs=pl.BlockSpec(last.shape, lambda i: (row, 0, 0)),
        input_output_aliases={0: 0},
    )(basis_ext, last)


def tendency(concen, coeffs, diff_scale):
    velocity = coeffs[:3]
    kappa = coeffs[3]
    center = concen[:, 2:-2, 2:-2, :]
    flux_first = velocity[0][None] * concen
    slope = (
        8.0 * (flux_first[:, 3:-1, 2:-2] - flux_first[:, 1:-3, 2:-2])
        - (flux_first[:, 4:, 2:-2] - flux_first[:, :-4, 2:-2])
    ) / 12.0
    flux_second = velocity[1][None] * concen
    slope = (
        slope
        + (
            8.0 * (flux_second[:, 2:-2, 3:-1] - flux_second[:, 2:-2, 1:-3])
            - (flux_second[:, 2:-2, 4:] - flux_second[:, 2:-2, :-4])
        )
        / 12.0
    )
    flux_third = jnp.pad(velocity[2][2:-2, 2:-2][None] * center, ((0, 0), (0, 0), (0, 0), (2, 2)))
    slope = (
        slope
        + (
            8.0 * (flux_third[..., 3:-1] - flux_third[..., 1:-3])
            - (flux_third[..., 4:] - flux_third[..., :-4])
        )
        / 12.0
    )
    kappa_mid = kappa[2:-2, 2:-2][None]
    spread = (kappa_mid + kappa[3:-1, 2:-2][None]) * 0.5 * (concen[:, 3:-1, 2:-2] - center) - (
        kappa_mid + kappa[1:-3, 2:-2][None]
    ) * 0.5 * (center - concen[:, 1:-3, 2:-2])
    spread = (
        spread
        + (kappa_mid + kappa[2:-2, 3:-1][None]) * 0.5 * (concen[:, 2:-2, 3:-1] - center)
        - (kappa_mid + kappa[2:-2, 1:-3][None]) * 0.5 * (center - concen[:, 2:-2, 1:-3])
    )
    kappa_pad = jnp.pad(kappa_mid, ((0, 0), (0, 0), (0, 0), (1, 1)))
    center_pad = jnp.pad(center, ((0, 0), (0, 0), (0, 0), (1, 1)))
    spread = (
        spread
        + (kappa_mid + kappa_pad[..., 2:]) * 0.5 * (center_pad[..., 2:] - center)
        - (kappa_mid + kappa_pad[..., :-2]) * 0.5 * (center - center_pad[..., :-2])
    )
    return center + time_step * (diff_scale[:, None, None, None] * spread - slope)


def stencil_body(scale_ref, conc_ref, coeff_ref, out_ref):
    s = pl.program_id(0)
    scale = scale_ref[s]
    rows = out_ref.shape[2]
    depth = out_ref.shape[3]
    lane = lax.broadcasted_iota(jnp.int32, (rows, depth), 1)

    def shifted(value, d):
        rolled = pltpu.roll(value, (-d) % depth, 1)
        keep = (lane + d >= 0) & (lane + d < depth)
        return jnp.where(keep, rolled, 0.0)

    def row(i, carry):
        def c(dx, dy):
            return conc_ref[0, i + 2 + dx, pl.ds(2 + dy, rows), :]

        def k(field, dx, dy):
            return coeff_ref[field, i + 2 + dx, pl.ds(2 + dy, rows), :]

        center = c(0, 0)

        def f1(d):
            return k(0, d, 0) * c(d, 0)

        slope = 8.0 * (f1(1) - f1(-1)) - (f1(2) - f1(-2))

        def f2(d):
            return k(1, 0, d) * c(0, d)

        slope = slope + (8.0 * (f2(1) - f2(-1)) - (f2(2) - f2(-2)))
        f3 = k(2, 0, 0) * center
        slope = slope + (
            8.0 * (shifted(f3, 1) - shifted(f3, -1)) - (shifted(f3, 2) - shifted(f3, -2))
        )
        slope = slope * (1.0 / 12.0)
        kmid = k(3, 0, 0)
        spread = (kmid + k(3, 1, 0)) * 0.5 * (c(1, 0) - center) - (kmid + k(3, -1, 0)) * 0.5 * (
            center - c(-1, 0)
        )
        spread = (
            spread
            + (kmid + k(3, 0, 1)) * 0.5 * (c(0, 1) - center)
            - (kmid + k(3, 0, -1)) * 0.5 * (center - c(0, -1))
        )
        spread = (
            spread
            + (kmid + shifted(kmid, 1)) * 0.5 * (shifted(center, 1) - center)
            - (kmid + shifted(kmid, -1)) * 0.5 * (center - shifted(center, -1))
        )
        out_ref[0, i] = center + time_step * (scale * spread - slope)
        return carry

    lax.fori_loop(0, out_ref.shape[1], row, 0, unroll=8)


def stencil_step(conc_pad, coeff_pad, scale):
    count, px, py, depth = conc_pad.shape
    nx, ny = px - 4, py - 4
    return pl.pallas_call(
        stencil_body,
        out_shape=jax.ShapeDtypeStruct((count, nx, ny, depth), jnp.float32),
        grid=(count,),
        in_specs=[
            pl.BlockSpec(memory_space=pltpu.SMEM),
            pl.BlockSpec((1, px, py, depth), lambda s: (s, 0, 0, 0)),
            pl.BlockSpec(coeff_pad.shape, lambda s: (0, 0, 0, 0)),
        ],
        out_specs=pl.BlockSpec((1, nx, ny, depth), lambda s: (s, 0, 0, 0)),
        compiler_params=pltpu.CompilerParams(vmem_limit_bytes=48 * 1024 * 1024),
        cost_estimate=pl.CostEstimate(
            flops=80 * count * nx * ny * depth,
            transcendentals=0,
            bytes_accessed=4 * (conc_pad.size + coeff_pad.size + count * nx * ny * depth),
        ),
    )(scale, conc_pad, coeff_pad)


def basis_body(mix_ref, xt_ref, out_ref):
    for a in range(xt_ref.shape[0]):
        xa = xt_ref[a]
        res = jnp.dot(mix_ref[0], xa, preferred_element_type=jnp.float32)
        res = res + jnp.dot(mix_ref[1], xa, preferred_element_type=jnp.float32)
        res = res + jnp.dot(mix_ref[2], xa, preferred_element_type=jnp.float32)
        out_ref[:, a, :] = res


def basis_rows(mix_ext, static):
    hi = lax.reduce_precision(mix_ext, exponent_bits=8, mantissa_bits=7)
    rem = mix_ext - hi
    mid = lax.reduce_precision(rem, exponent_bits=8, mantissa_bits=7)
    lo = rem - mid
    parts = jnp.stack([hi, mid, lo], 0).astype(jnp.bfloat16)
    xt = jnp.transpose(static, (1, 0, 2))
    span, width, cols = xt.shape
    rows = mix_ext.shape[0]
    block = 8
    return pl.pallas_call(
        basis_body,
        out_shape=jax.ShapeDtypeStruct((rows, span, cols), jnp.float32),
        grid=(span // block,),
        in_specs=[
            pl.BlockSpec(parts.shape, lambda i: (0, 0, 0)),
            pl.BlockSpec((block, width, cols), lambda i: (i, 0, 0)),
        ],
        out_specs=pl.BlockSpec((rows, block, cols), lambda i: (0, i, 0)),
        compiler_params=pltpu.CompilerParams(vmem_limit_bytes=48 * 1024 * 1024),
        cost_estimate=pl.CostEstimate(
            flops=6 * rows * width * span * cols,
            transcendentals=0,
            bytes_accessed=2 * xt.size + 4 * rows * span * cols,
        ),
    )(parts, xt)


def per_device(scalars, velocity, diffusivity, diff_scale, basis_old, sing_values, stored):
    rank = basis_old.shape[0]
    snaps = stored.shape[0]
    static = jnp.concatenate([basis_old, stored], 0)
    weight = jnp.concatenate([sing_values, jnp.ones((snaps,), jnp.float32)], 0)
    total_rows = static.shape[1] * static.shape[2] * lax.axis_size("gx") * lax.axis_size("gy")

    local_gram = lax.dot_general(
        static, static, (((1, 2), (1, 2)), ((), ())), preferred_element_type=jnp.float32
    )
    coeffs = jnp.concatenate([velocity, diffusivity[None]], 0)
    count = scalars.shape[0]
    first = halo(jnp.concatenate([scalars, coeffs], 0))
    coeff_pad = first[count:]
    middle0 = stencil_step(first[:1], coeff_pad, diff_scale[:1])
    local_gram, middle0 = lax.optimization_barrier((local_gram, middle0))
    gram_static = butterfly_sum(local_gram) * (weight[:, None] * weight[None, :]) / total_rows
    lower_static = jnp.linalg.cholesky(gram_static)
    width = rank + snaps
    inv_static = lax.linalg.triangular_solve(
        lower_static, jnp.eye(width, dtype=jnp.float32), left_side=True, lower=True
    )
    mix = inv_static * weight[None, :]
    mix_ext = jnp.concatenate([mix, jnp.zeros((1, width), jnp.float32)], 0)
    basis_ext = basis_rows(mix_ext, static)

    result0 = stencil_step(halo(middle0), coeff_pad, diff_scale[:1])

    coarse = result0[0, ::2]
    span, depth = coarse.shape[1], coarse.shape[2]
    pick_z = (jnp.arange(depth)[:, None] == 2 * jnp.arange(depth // 2)[None, :]).astype(jnp.float32)
    pick_y = (2 * jnp.arange(span // 2)[:, None] == jnp.arange(span)[None, :]).astype(jnp.float32)
    thin = jnp.einsum("ayz,zk->ayk", coarse, pick_z, precision=lax.Precision.HIGHEST)
    fresh = jnp.einsum("jy,ayk->ajk", pick_y, thin, precision=lax.Precision.HIGHEST).reshape(
        coarse.shape[0], -1
    )
    static_f32 = static.astype(jnp.float32)
    cross = jnp.sum(static_f32 * fresh[None], axis=(1, 2))
    self_dot = jnp.sum(fresh * fresh)
    moments = butterfly_sum(jnp.concatenate([cross, self_dot[None]], 0)) / total_rows
    cross_g = moments[:width] * weight
    self_g = moments[width]

    middle_r = stencil_step(first[1:count], coeff_pad, diff_scale[1:])
    result_r = stencil_step(halo(middle_r), coeff_pad, diff_scale[1:])
    result = jnp.concatenate([result0, result_r], 0)

    link = lax.linalg.triangular_solve(
        lower_static, cross_g[:, None], left_side=True, lower=True
    )[:, 0]
    corner = jnp.sqrt(self_g - jnp.sum(link * link))
    lower = jnp.zeros((width + 1, width + 1), jnp.float32)
    lower = lower.at[:width, :width].set(lower_static)
    lower = lower.at[width, :width].set(link)
    lower = lower.at[width, width].set(corner)

    along = jnp.sum(mix * link[:, None], axis=0)
    last = (fresh - jnp.sum(static_f32 * along[:, None, None], axis=0)) / corner
    basis_new = put_last_row(basis_ext, last.reshape((1,) + basis_ext.shape[1:]))
    return (result, basis_new, lower.T)


def solution(mesh):
    return jax.shard_map(
        per_device,
        mesh=mesh,
        in_specs=(
            P(None, "gx", "gy", None),
            P(None, "gx", "gy", None),
            P("gx", "gy", None),
            P(),
            P(None, "gx", "gy"),
            P(),
            P(None, "gx", "gy"),
        ),
        out_specs=(P(None, "gx", "gy", None), P(None, "gx", "gy"), P()),
        check_vma=False,
    )
```

```python
import jax
import jax.numpy as jnp
from jax import lax
from jax.sharding import PartitionSpec as P
from jax.experimental import pallas as pl
from jax.experimental.pallas import tpu as pltpu

time_step = 0.25


def ring(axis):
    count = lax.axis_size(axis)
    forward = [(i, (i + 1) % count) for i in range(count)]
    backward = [(target, source) for source, target in forward]
    return forward, backward


def halo(block, width=2):
    fx, bx = ring("gx")
    fy, by = ring("gy")
    nx, ny = block.shape[1], block.shape[2]
    low_x = lax.ppermute(block[:, nx - width :], "gx", fx)
    high_x = lax.ppermute(block[:, :width], "gx", bx)
    low_y = lax.ppermute(block[:, :, ny - width :], "gy", fy)
    high_y = lax.ppermute(block[:, :, :width], "gy", by)
    rows = jnp.concatenate([low_x, block, high_x], axis=1)
    edge = ((0, 0), (width, width), (0, 0), (0, 0))
    return jnp.concatenate([jnp.pad(low_y, edge), rows, jnp.pad(high_y, edge)], axis=2)


def butterfly_sum(value):
    for axis in ("gx", "gy"):
        count = lax.axis_size(axis)
        bit = 1
        while bit < count:
            pairs = [(i, i ^ bit) for i in range(count)]
            value = value + lax.ppermute(value, axis, pairs)
            bit *= 2
    return value


def put_last_row(basis_ext, last):
    def body(_, last_ref, out_ref):
        out_ref[...] = last_ref[...]

    row = basis_ext.shape[0] - 1
    return pl.pallas_call(
        body,
        out_shape=jax.ShapeDtypeStruct(basis_ext.shape, basis_ext.dtype),
        grid=(1,),
        in_specs=[pl.BlockSpec(memory_space=pl.ANY), pl.BlockSpec(last.shape, lambda i: (0, 0, 0))],
        out_specs=pl.BlockSpec(last.shape, lambda i: (row, 0, 0)),
        input_output_aliases={0: 0},
    )(basis_ext, last)


def tendency(concen, coeffs, diff_scale):
    velocity = coeffs[:3]
    kappa = coeffs[3]
    center = concen[:, 2:-2, 2:-2, :]
    flux_first = velocity[0][None] * concen
    slope = (
        8.0 * (flux_first[:, 3:-1, 2:-2] - flux_first[:, 1:-3, 2:-2])
        - (flux_first[:, 4:, 2:-2] - flux_first[:, :-4, 2:-2])
    ) / 12.0
    flux_second = velocity[1][None] * concen
    slope = (
        slope
        + (
            8.0 * (flux_second[:, 2:-2, 3:-1] - flux_second[:, 2:-2, 1:-3])
            - (flux_second[:, 2:-2, 4:] - flux_second[:, 2:-2, :-4])
        )
        / 12.0
    )
    flux_third = jnp.pad(velocity[2][2:-2, 2:-2][None] * center, ((0, 0), (0, 0), (0, 0), (2, 2)))
    slope = (
        slope
        + (
            8.0 * (flux_third[..., 3:-1] - flux_third[..., 1:-3])
            - (flux_third[..., 4:] - flux_third[..., :-4])
        )
        / 12.0
    )
    kappa_mid = kappa[2:-2, 2:-2][None]
    spread = (kappa_mid + kappa[3:-1, 2:-2][None]) * 0.5 * (concen[:, 3:-1, 2:-2] - center) - (
        kappa_mid + kappa[1:-3, 2:-2][None]
    ) * 0.5 * (center - concen[:, 1:-3, 2:-2])
    spread = (
        spread
        + (kappa_mid + kappa[2:-2, 3:-1][None]) * 0.5 * (concen[:, 2:-2, 3:-1] - center)
        - (kappa_mid + kappa[2:-2, 1:-3][None]) * 0.5 * (center - concen[:, 2:-2, 1:-3])
    )
    kappa_pad = jnp.pad(kappa_mid, ((0, 0), (0, 0), (0, 0), (1, 1)))
    center_pad = jnp.pad(center, ((0, 0), (0, 0), (0, 0), (1, 1)))
    spread = (
        spread
        + (kappa_mid + kappa_pad[..., 2:]) * 0.5 * (center_pad[..., 2:] - center)
        - (kappa_mid + kappa_pad[..., :-2]) * 0.5 * (center - center_pad[..., :-2])
    )
    return center + time_step * (diff_scale[:, None, None, None] * spread - slope)


def stencil_body(scale_ref, conc_ref, coeff_ref, out_ref):
    s = pl.program_id(0)
    scale = scale_ref[s]
    rows = out_ref.shape[2]
    depth = out_ref.shape[3]
    lane = lax.broadcasted_iota(jnp.int32, (rows, depth), 1)

    def shifted(value, d):
        rolled = pltpu.roll(value, (-d) % depth, 1)
        keep = (lane + d >= 0) & (lane + d < depth)
        return jnp.where(keep, rolled, 0.0)

    def row(i, carry):
        def c(dx, dy):
            return conc_ref[0, i + 2 + dx, pl.ds(2 + dy, rows), :]

        def k(field, dx, dy):
            return coeff_ref[field, i + 2 + dx, pl.ds(2 + dy, rows), :]

        center = c(0, 0)

        def f1(d):
            return k(0, d, 0) * c(d, 0)

        slope = 8.0 * (f1(1) - f1(-1)) - (f1(2) - f1(-2))

        def f2(d):
            return k(1, 0, d) * c(0, d)

        slope = slope + (8.0 * (f2(1) - f2(-1)) - (f2(2) - f2(-2)))
        f3 = k(2, 0, 0) * center
        slope = slope + (
            8.0 * (shifted(f3, 1) - shifted(f3, -1)) - (shifted(f3, 2) - shifted(f3, -2))
        )
        slope = slope * (1.0 / 12.0)
        kmid = k(3, 0, 0)
        spread = (kmid + k(3, 1, 0)) * 0.5 * (c(1, 0) - center) - (kmid + k(3, -1, 0)) * 0.5 * (
            center - c(-1, 0)
        )
        spread = (
            spread
            + (kmid + k(3, 0, 1)) * 0.5 * (c(0, 1) - center)
            - (kmid + k(3, 0, -1)) * 0.5 * (center - c(0, -1))
        )
        spread = (
            spread
            + (kmid + shifted(kmid, 1)) * 0.5 * (shifted(center, 1) - center)
            - (kmid + shifted(kmid, -1)) * 0.5 * (center - shifted(center, -1))
        )
        out_ref[0, i] = center + time_step * (scale * spread - slope)
        return carry

    lax.fori_loop(0, out_ref.shape[1], row, 0, unroll=16)


def stencil_step(conc_pad, coeff_pad, scale):
    count, px, py, depth = conc_pad.shape
    nx, ny = px - 4, py - 4
    return pl.pallas_call(
        stencil_body,
        out_shape=jax.ShapeDtypeStruct((count, nx, ny, depth), jnp.float32),
        grid=(count,),
        in_specs=[
            pl.BlockSpec(memory_space=pltpu.SMEM),
            pl.BlockSpec((1, px, py, depth), lambda s: (s, 0, 0, 0)),
            pl.BlockSpec(coeff_pad.shape, lambda s: (0, 0, 0, 0)),
        ],
        out_specs=pl.BlockSpec((1, nx, ny, depth), lambda s: (s, 0, 0, 0)),
        compiler_params=pltpu.CompilerParams(vmem_limit_bytes=48 * 1024 * 1024),
        cost_estimate=pl.CostEstimate(
            flops=80 * count * nx * ny * depth,
            transcendentals=0,
            bytes_accessed=4 * (conc_pad.size + coeff_pad.size + count * nx * ny * depth),
        ),
    )(scale, conc_pad, coeff_pad)


def basis_body(mix_ref, xt_ref, out_ref):
    for a in range(xt_ref.shape[0]):
        xa = xt_ref[a]
        res = jnp.dot(mix_ref[0], xa, preferred_element_type=jnp.float32)
        res = res + jnp.dot(mix_ref[1], xa, preferred_element_type=jnp.float32)
        res = res + jnp.dot(mix_ref[2], xa, preferred_element_type=jnp.float32)
        out_ref[:, a, :] = res


def basis_rows(mix_ext, static):
    hi = lax.reduce_precision(mix_ext, exponent_bits=8, mantissa_bits=7)
    rem = mix_ext - hi
    mid = lax.reduce_precision(rem, exponent_bits=8, mantissa_bits=7)
    lo = rem - mid
    parts = jnp.stack([hi, mid, lo], 0).astype(jnp.bfloat16)
    xt = jnp.transpose(static, (1, 0, 2))
    span, width, cols = xt.shape
    rows = mix_ext.shape[0]
    block = 8
    return pl.pallas_call(
        basis_body,
        out_shape=jax.ShapeDtypeStruct((rows, span, cols), jnp.float32),
        grid=(span // block,),
        in_specs=[
            pl.BlockSpec(parts.shape, lambda i: (0, 0, 0)),
            pl.BlockSpec((block, width, cols), lambda i: (i, 0, 0)),
        ],
        out_specs=pl.BlockSpec((rows, block, cols), lambda i: (0, i, 0)),
        compiler_params=pltpu.CompilerParams(vmem_limit_bytes=48 * 1024 * 1024),
        cost_estimate=pl.CostEstimate(
            flops=6 * rows * width * span * cols,
            transcendentals=0,
            bytes_accessed=2 * xt.size + 4 * rows * span * cols,
        ),
    )(parts, xt)


def per_device(scalars, velocity, diffusivity, diff_scale, basis_old, sing_values, stored):
    rank = basis_old.shape[0]
    snaps = stored.shape[0]
    static = jnp.concatenate([basis_old, stored], 0)
    weight = jnp.concatenate([sing_values, jnp.ones((snaps,), jnp.float32)], 0)
    total_rows = static.shape[1] * static.shape[2] * lax.axis_size("gx") * lax.axis_size("gy")

    local_gram = lax.dot_general(
        static, static, (((1, 2), (1, 2)), ((), ())), preferred_element_type=jnp.float32
    )
    coeffs = jnp.concatenate([velocity, diffusivity[None]], 0)
    count = scalars.shape[0]
    first = halo(jnp.concatenate([scalars, coeffs], 0))
    coeff_pad = first[count:]
    middle0 = stencil_step(first[:1], coeff_pad, diff_scale[:1])
    local_gram, middle0 = lax.optimization_barrier((local_gram, middle0))
    gram_static = butterfly_sum(local_gram) * (weight[:, None] * weight[None, :]) / total_rows
    lower_static = jnp.linalg.cholesky(gram_static)
    width = rank + snaps
    inv_static = lax.linalg.triangular_solve(
        lower_static, jnp.eye(width, dtype=jnp.float32), left_side=True, lower=True
    )
    mix = inv_static * weight[None, :]
    mix_ext = jnp.concatenate([mix, jnp.zeros((1, width), jnp.float32)], 0)
    basis_ext = basis_rows(mix_ext, static)

    result0 = stencil_step(halo(middle0), coeff_pad, diff_scale[:1])

    coarse = result0[0, ::2]
    span, depth = coarse.shape[1], coarse.shape[2]
    pick_z = (jnp.arange(depth)[:, None] == 2 * jnp.arange(depth // 2)[None, :]).astype(jnp.float32)
    pick_y = (2 * jnp.arange(span // 2)[:, None] == jnp.arange(span)[None, :]).astype(jnp.float32)
    thin = jnp.einsum("ayz,zk->ayk", coarse, pick_z, precision=lax.Precision.HIGHEST)
    fresh = jnp.einsum("jy,ayk->ajk", pick_y, thin, precision=lax.Precision.HIGHEST).reshape(
        coarse.shape[0], -1
    )
    static_f32 = static.astype(jnp.float32)
    cross = jnp.sum(static_f32 * fresh[None], axis=(1, 2))
    self_dot = jnp.sum(fresh * fresh)
    moments = butterfly_sum(jnp.concatenate([cross, self_dot[None]], 0)) / total_rows
    cross_g = moments[:width] * weight
    self_g = moments[width]

    middle_r = stencil_step(first[1:count], coeff_pad, diff_scale[1:])
    result_r = stencil_step(halo(middle_r), coeff_pad, diff_scale[1:])
    result = jnp.concatenate([result0, result_r], 0)

    link = lax.linalg.triangular_solve(
        lower_static, cross_g[:, None], left_side=True, lower=True
    )[:, 0]
    corner = jnp.sqrt(self_g - jnp.sum(link * link))
    lower = jnp.zeros((width + 1, width + 1), jnp.float32)
    lower = lower.at[:width, :width].set(lower_static)
    lower = lower.at[width, :width].set(link)
    lower = lower.at[width, width].set(corner)

    along = jnp.sum(mix * link[:, None], axis=0)
    last = (fresh - jnp.sum(static_f32 * along[:, None, None], axis=0)) / corner
    basis_new = put_last_row(basis_ext, last.reshape((1,) + basis_ext.shape[1:]))
    return (result, basis_new, lower.T)


def solution(mesh):
    return jax.shard_map(
        per_device,
        mesh=mesh,
        in_specs=(
            P(None, "gx", "gy", None),
            P(None, "gx", "gy", None),
            P("gx", "gy", None),
            P(),
            P(None, "gx", "gy"),
            P(),
            P(None, "gx", "gy"),
        ),
        out_specs=(P(None, "gx", "gy", None), P(None, "gx", "gy"), P()),
        check_vma=False,
    )
```

```python
import jax
import jax.numpy as jnp
from jax import lax
from jax.sharding import PartitionSpec as P
from jax.experimental import pallas as pl
from jax.experimental.pallas import tpu as pltpu

time_step = 0.25


def ring(axis):
    count = lax.axis_size(axis)
    forward = [(i, (i + 1) % count) for i in range(count)]
    backward = [(target, source) for source, target in forward]
    return forward, backward


def halo(block, width=2):
    fx, bx = ring("gx")
    fy, by = ring("gy")
    nx, ny = block.shape[1], block.shape[2]
    low_x = lax.ppermute(block[:, nx - width :], "gx", fx)
    high_x = lax.ppermute(block[:, :width], "gx", bx)
    low_y = lax.ppermute(block[:, :, ny - width :], "gy", fy)
    high_y = lax.ppermute(block[:, :, :width], "gy", by)
    rows = jnp.concatenate([low_x, block, high_x], axis=1)
    edge = ((0, 0), (width, width), (0, 0), (0, 0))
    return jnp.concatenate([jnp.pad(low_y, edge), rows, jnp.pad(high_y, edge)], axis=2)


def butterfly_sum(value):
    for axis in ("gx", "gy"):
        count = lax.axis_size(axis)
        bit = 1
        while bit < count:
            pairs = [(i, i ^ bit) for i in range(count)]
            value = value + lax.ppermute(value, axis, pairs)
            bit *= 2
    return value


def put_last_row(basis_ext, last):
    def body(_, last_ref, out_ref):
        out_ref[...] = last_ref[...]

    row = basis_ext.shape[0] - 1
    return pl.pallas_call(
        body,
        out_shape=jax.ShapeDtypeStruct(basis_ext.shape, basis_ext.dtype),
        grid=(1,),
        in_specs=[pl.BlockSpec(memory_space=pl.ANY), pl.BlockSpec(last.shape, lambda i: (0, 0, 0))],
        out_specs=pl.BlockSpec(last.shape, lambda i: (row, 0, 0)),
        input_output_aliases={0: 0},
    )(basis_ext, last)


def tendency(concen, coeffs, diff_scale):
    velocity = coeffs[:3]
    kappa = coeffs[3]
    center = concen[:, 2:-2, 2:-2, :]
    flux_first = velocity[0][None] * concen
    slope = (
        8.0 * (flux_first[:, 3:-1, 2:-2] - flux_first[:, 1:-3, 2:-2])
        - (flux_first[:, 4:, 2:-2] - flux_first[:, :-4, 2:-2])
    ) / 12.0
    flux_second = velocity[1][None] * concen
    slope = (
        slope
        + (
            8.0 * (flux_second[:, 2:-2, 3:-1] - flux_second[:, 2:-2, 1:-3])
            - (flux_second[:, 2:-2, 4:] - flux_second[:, 2:-2, :-4])
        )
        / 12.0
    )
    flux_third = jnp.pad(velocity[2][2:-2, 2:-2][None] * center, ((0, 0), (0, 0), (0, 0), (2, 2)))
    slope = (
        slope
        + (
            8.0 * (flux_third[..., 3:-1] - flux_third[..., 1:-3])
            - (flux_third[..., 4:] - flux_third[..., :-4])
        )
        / 12.0
    )
    kappa_mid = kappa[2:-2, 2:-2][None]
    spread = (kappa_mid + kappa[3:-1, 2:-2][None]) * 0.5 * (concen[:, 3:-1, 2:-2] - center) - (
        kappa_mid + kappa[1:-3, 2:-2][None]
    ) * 0.5 * (center - concen[:, 1:-3, 2:-2])
    spread = (
        spread
        + (kappa_mid + kappa[2:-2, 3:-1][None]) * 0.5 * (concen[:, 2:-2, 3:-1] - center)
        - (kappa_mid + kappa[2:-2, 1:-3][None]) * 0.5 * (center - concen[:, 2:-2, 1:-3])
    )
    kappa_pad = jnp.pad(kappa_mid, ((0, 0), (0, 0), (0, 0), (1, 1)))
    center_pad = jnp.pad(center, ((0, 0), (0, 0), (0, 0), (1, 1)))
    spread = (
        spread
        + (kappa_mid + kappa_pad[..., 2:]) * 0.5 * (center_pad[..., 2:] - center)
        - (kappa_mid + kappa_pad[..., :-2]) * 0.5 * (center - center_pad[..., :-2])
    )
    return center + time_step * (diff_scale[:, None, None, None] * spread - slope)


def stencil_body(scale_ref, conc_ref, coeff_ref, out_ref):
    s = pl.program_id(0)
    scale = scale_ref[s]
    rows = out_ref.shape[2]
    depth = out_ref.shape[3]
    lane = lax.broadcasted_iota(jnp.int32, (rows, depth), 1)

    def shifted(value, d):
        rolled = pltpu.roll(value, (-d) % depth, 1)
        keep = (lane + d >= 0) & (lane + d < depth)
        return jnp.where(keep, rolled, 0.0)

    def row(i, carry):
        def c(dx, dy):
            return conc_ref[0, i + 2 + dx, pl.ds(2 + dy, rows), :]

        def k(field, dx, dy):
            return coeff_ref[field, i + 2 + dx, pl.ds(2 + dy, rows), :]

        center = c(0, 0)

        def f1(d):
            return k(0, d, 0) * c(d, 0)

        slope = 8.0 * (f1(1) - f1(-1)) - (f1(2) - f1(-2))

        def f2(d):
            return k(1, 0, d) * c(0, d)

        slope = slope + (8.0 * (f2(1) - f2(-1)) - (f2(2) - f2(-2)))
        f3 = k(2, 0, 0) * center
        slope = slope + (
            8.0 * (shifted(f3, 1) - shifted(f3, -1)) - (shifted(f3, 2) - shifted(f3, -2))
        )
        slope = slope * (1.0 / 12.0)
        kmid = k(3, 0, 0)
        spread = (kmid + k(3, 1, 0)) * 0.5 * (c(1, 0) - center) - (kmid + k(3, -1, 0)) * 0.5 * (
            center - c(-1, 0)
        )
        spread = (
            spread
            + (kmid + k(3, 0, 1)) * 0.5 * (c(0, 1) - center)
            - (kmid + k(3, 0, -1)) * 0.5 * (center - c(0, -1))
        )
        spread = (
            spread
            + (kmid + shifted(kmid, 1)) * 0.5 * (shifted(center, 1) - center)
            - (kmid + shifted(kmid, -1)) * 0.5 * (center - shifted(center, -1))
        )
        out_ref[0, i] = center + time_step * (scale * spread - slope)
        return carry

    lax.fori_loop(0, out_ref.shape[1], row, 0, unroll=16)


def stencil_step(conc_pad, start, count, coeff_pad, scale):
    _, px, py, depth = conc_pad.shape
    fields = 4
    assert (coeff_pad.shape[0] - fields) % fields == 0
    coeff_block = (coeff_pad.shape[0] - fields) // fields
    nx, ny = px - 4, py - 4
    return pl.pallas_call(
        stencil_body,
        out_shape=jax.ShapeDtypeStruct((count, nx, ny, depth), jnp.float32),
        grid=(count,),
        in_specs=[
            pl.BlockSpec(memory_space=pltpu.SMEM),
            pl.BlockSpec((1, px, py, depth), lambda s: (s + start, 0, 0, 0)),
            pl.BlockSpec((fields, px, py, depth), lambda s: (coeff_block, 0, 0, 0)),
        ],
        out_specs=pl.BlockSpec((1, nx, ny, depth), lambda s: (s, 0, 0, 0)),
        compiler_params=pltpu.CompilerParams(vmem_limit_bytes=48 * 1024 * 1024),
        cost_estimate=pl.CostEstimate(
            flops=80 * count * nx * ny * depth,
            transcendentals=0,
            bytes_accessed=4 * (2 * count + fields) * px * py * depth,
        ),
    )(scale, conc_pad, coeff_pad)


def basis_body(mix_ref, xt_ref, out_ref):
    for a in range(xt_ref.shape[0]):
        xa = xt_ref[a]
        res = jnp.dot(mix_ref[0], xa, preferred_element_type=jnp.float32)
        res = res + jnp.dot(mix_ref[1], xa, preferred_element_type=jnp.float32)
        res = res + jnp.dot(mix_ref[2], xa, preferred_element_type=jnp.float32)
        out_ref[:, a, :] = res


def basis_rows(mix_ext, static):
    hi = lax.reduce_precision(mix_ext, exponent_bits=8, mantissa_bits=7)
    rem = mix_ext - hi
    mid = lax.reduce_precision(rem, exponent_bits=8, mantissa_bits=7)
    lo = rem - mid
    parts = jnp.stack([hi, mid, lo], 0).astype(jnp.bfloat16)
    xt = jnp.transpose(static, (1, 0, 2))
    span, width, cols = xt.shape
    rows = mix_ext.shape[0]
    block = 8
    return pl.pallas_call(
        basis_body,
        out_shape=jax.ShapeDtypeStruct((rows, span, cols), jnp.float32),
        grid=(span // block,),
        in_specs=[
            pl.BlockSpec(parts.shape, lambda i: (0, 0, 0)),
            pl.BlockSpec((block, width, cols), lambda i: (i, 0, 0)),
        ],
        out_specs=pl.BlockSpec((rows, block, cols), lambda i: (0, i, 0)),
        compiler_params=pltpu.CompilerParams(vmem_limit_bytes=48 * 1024 * 1024),
        cost_estimate=pl.CostEstimate(
            flops=6 * rows * width * span * cols,
            transcendentals=0,
            bytes_accessed=2 * xt.size + 4 * rows * span * cols,
        ),
    )(parts, xt)


def per_device(scalars, velocity, diffusivity, diff_scale, basis_old, sing_values, stored):
    rank = basis_old.shape[0]
    snaps = stored.shape[0]
    static = jnp.concatenate([basis_old, stored], 0)
    weight = jnp.concatenate([sing_values, jnp.ones((snaps,), jnp.float32)], 0)
    total_rows = static.shape[1] * static.shape[2] * lax.axis_size("gx") * lax.axis_size("gy")

    local_gram = lax.dot_general(
        static, static, (((1, 2), (1, 2)), ((), ())), preferred_element_type=jnp.float32
    )
    coeffs = jnp.concatenate([velocity, diffusivity[None]], 0)
    count = scalars.shape[0]
    first = halo(jnp.concatenate([scalars, coeffs], 0))
    middle0 = stencil_step(first, 0, 1, first, diff_scale[:1])
    local_gram, middle0 = lax.optimization_barrier((local_gram, middle0))
    gram_static = butterfly_sum(local_gram) * (weight[:, None] * weight[None, :]) / total_rows
    lower_static = jnp.linalg.cholesky(gram_static)
    width = rank + snaps
    inv_static = lax.linalg.triangular_solve(
        lower_static, jnp.eye(width, dtype=jnp.float32), left_side=True, lower=True
    )
    mix = inv_static * weight[None, :]
    mix_ext = jnp.concatenate([mix, jnp.zeros((1, width), jnp.float32)], 0)
    basis_ext = basis_rows(mix_ext, static)

    result0 = stencil_step(halo(middle0), 0, 1, first, diff_scale[:1])

    coarse = result0[0, ::2]
    span, depth = coarse.shape[1], coarse.shape[2]
    pick_z = (jnp.arange(depth)[:, None] == 2 * jnp.arange(depth // 2)[None, :]).astype(jnp.float32)
    pick_y = (2 * jnp.arange(span // 2)[:, None] == jnp.arange(span)[None, :]).astype(jnp.float32)
    thin = jnp.einsum("ayz,zk->ayk", coarse, pick_z, precision=lax.Precision.HIGHEST)
    fresh = jnp.einsum("jy,ayk->ajk", pick_y, thin, precision=lax.Precision.HIGHEST).reshape(
        coarse.shape[0], -1
    )
    static_f32 = static.astype(jnp.float32)
    cross = jnp.sum(static_f32 * fresh[None], axis=(1, 2))
    self_dot = jnp.sum(fresh * fresh)
    moments = butterfly_sum(jnp.concatenate([cross, self_dot[None]], 0)) / total_rows
    cross_g = moments[:width] * weight
    self_g = moments[width]

    middle_r = stencil_step(first, 1, count - 1, first, diff_scale[1:])
    result_r = stencil_step(halo(middle_r), 0, count - 1, first, diff_scale[1:])
    result = jnp.concatenate([result0, result_r], 0)

    link = lax.linalg.triangular_solve(
        lower_static, cross_g[:, None], left_side=True, lower=True
    )[:, 0]
    corner = jnp.sqrt(self_g - jnp.sum(link * link))
    lower = jnp.zeros((width + 1, width + 1), jnp.float32)
    lower = lower.at[:width, :width].set(lower_static)
    lower = lower.at[width, :width].set(link)
    lower = lower.at[width, width].set(corner)

    along = jnp.sum(mix * link[:, None], axis=0)
    last = (fresh - jnp.sum(static_f32 * along[:, None, None], axis=0)) / corner
    basis_new = put_last_row(basis_ext, last.reshape((1,) + basis_ext.shape[1:]))
    return (result, basis_new, lower.T)


def solution(mesh):
    return jax.shard_map(
        per_device,
        mesh=mesh,
        in_specs=(
            P(None, "gx", "gy", None),
            P(None, "gx", "gy", None),
            P("gx", "gy", None),
            P(),
            P(None, "gx", "gy"),
            P(),
            P(None, "gx", "gy"),
        ),
        out_specs=(P(None, "gx", "gy", None), P(None, "gx", "gy"), P()),
        check_vma=False,
    )
```

```python
import jax
import jax.numpy as jnp
from jax import lax
from jax.sharding import PartitionSpec as P
from jax.experimental import pallas as pl
from jax.experimental.pallas import tpu as pltpu

time_step = 0.25


def ring(axis):
    count = lax.axis_size(axis)
    forward = [(i, (i + 1) % count) for i in range(count)]
    backward = [(target, source) for source, target in forward]
    return forward, backward


def halo(block, width=2):
    fx, bx = ring("gx")
    fy, by = ring("gy")
    nx, ny = block.shape[1], block.shape[2]
    low_x = lax.ppermute(block[:, nx - width :], "gx", fx)
    high_x = lax.ppermute(block[:, :width], "gx", bx)
    low_y = lax.ppermute(block[:, :, ny - width :], "gy", fy)
    high_y = lax.ppermute(block[:, :, :width], "gy", by)
    rows = jnp.concatenate([low_x, block, high_x], axis=1)
    edge = ((0, 0), (width, width), (0, 0), (0, 0))
    return jnp.concatenate([jnp.pad(low_y, edge), rows, jnp.pad(high_y, edge)], axis=2)


def butterfly_sum(value):
    for axis in ("gx", "gy"):
        count = lax.axis_size(axis)
        bit = 1
        while bit < count:
            pairs = [(i, i ^ bit) for i in range(count)]
            value = value + lax.ppermute(value, axis, pairs)
            bit *= 2
    return value


def put_last_row(basis_ext, last):
    def body(_, last_ref, out_ref):
        out_ref[...] = last_ref[...]

    row = basis_ext.shape[0] - 1
    return pl.pallas_call(
        body,
        out_shape=jax.ShapeDtypeStruct(basis_ext.shape, basis_ext.dtype),
        grid=(1,),
        in_specs=[pl.BlockSpec(memory_space=pl.ANY), pl.BlockSpec(last.shape, lambda i: (0, 0, 0))],
        out_specs=pl.BlockSpec(last.shape, lambda i: (row, 0, 0)),
        input_output_aliases={0: 0},
    )(basis_ext, last)


def tendency(concen, coeffs, diff_scale):
    velocity = coeffs[:3]
    kappa = coeffs[3]
    center = concen[:, 2:-2, 2:-2, :]
    flux_first = velocity[0][None] * concen
    slope = (
        8.0 * (flux_first[:, 3:-1, 2:-2] - flux_first[:, 1:-3, 2:-2])
        - (flux_first[:, 4:, 2:-2] - flux_first[:, :-4, 2:-2])
    ) / 12.0
    flux_second = velocity[1][None] * concen
    slope = (
        slope
        + (
            8.0 * (flux_second[:, 2:-2, 3:-1] - flux_second[:, 2:-2, 1:-3])
            - (flux_second[:, 2:-2, 4:] - flux_second[:, 2:-2, :-4])
        )
        / 12.0
    )
    flux_third = jnp.pad(velocity[2][2:-2, 2:-2][None] * center, ((0, 0), (0, 0), (0, 0), (2, 2)))
    slope = (
        slope
        + (
            8.0 * (flux_third[..., 3:-1] - flux_third[..., 1:-3])
            - (flux_third[..., 4:] - flux_third[..., :-4])
        )
        / 12.0
    )
    kappa_mid = kappa[2:-2, 2:-2][None]
    spread = (kappa_mid + kappa[3:-1, 2:-2][None]) * 0.5 * (concen[:, 3:-1, 2:-2] - center) - (
        kappa_mid + kappa[1:-3, 2:-2][None]
    ) * 0.5 * (center - concen[:, 1:-3, 2:-2])
    spread = (
        spread
        + (kappa_mid + kappa[2:-2, 3:-1][None]) * 0.5 * (concen[:, 2:-2, 3:-1] - center)
        - (kappa_mid + kappa[2:-2, 1:-3][None]) * 0.5 * (center - concen[:, 2:-2, 1:-3])
    )
    kappa_pad = jnp.pad(kappa_mid, ((0, 0), (0, 0), (0, 0), (1, 1)))
    center_pad = jnp.pad(center, ((0, 0), (0, 0), (0, 0), (1, 1)))
    spread = (
        spread
        + (kappa_mid + kappa_pad[..., 2:]) * 0.5 * (center_pad[..., 2:] - center)
        - (kappa_mid + kappa_pad[..., :-2]) * 0.5 * (center - center_pad[..., :-2])
    )
    return center + time_step * (diff_scale[:, None, None, None] * spread - slope)


def stencil_body(scale_ref, conc_ref, coeff_ref, out_ref):
    s = pl.program_id(0)
    scale = scale_ref[s]
    rows = out_ref.shape[2]
    depth = out_ref.shape[3]
    lane = lax.broadcasted_iota(jnp.int32, (rows, depth), 1)

    def shifted(value, d):
        rolled = pltpu.roll(value, (-d) % depth, 1)
        keep = (lane + d >= 0) & (lane + d < depth)
        return jnp.where(keep, rolled, 0.0)

    def row(i, carry):
        def c(dx, dy):
            return conc_ref[0, i + 2 + dx, pl.ds(2 + dy, rows), :]

        def k(field, dx, dy):
            return coeff_ref[field, i + 2 + dx, pl.ds(2 + dy, rows), :]

        center = c(0, 0)

        def f1(d):
            return k(0, d, 0) * c(d, 0)

        slope = 8.0 * (f1(1) - f1(-1)) - (f1(2) - f1(-2))

        def f2(d):
            return k(1, 0, d) * c(0, d)

        slope = slope + (8.0 * (f2(1) - f2(-1)) - (f2(2) - f2(-2)))
        f3 = k(2, 0, 0) * center
        slope = slope + (
            8.0 * (shifted(f3, 1) - shifted(f3, -1)) - (shifted(f3, 2) - shifted(f3, -2))
        )
        slope = slope * (1.0 / 12.0)
        kmid = k(3, 0, 0)
        spread = (kmid + k(3, 1, 0)) * 0.5 * (c(1, 0) - center) - (kmid + k(3, -1, 0)) * 0.5 * (
            center - c(-1, 0)
        )
        spread = (
            spread
            + (kmid + k(3, 0, 1)) * 0.5 * (c(0, 1) - center)
            - (kmid + k(3, 0, -1)) * 0.5 * (center - c(0, -1))
        )
        spread = (
            spread
            + (kmid + shifted(kmid, 1)) * 0.5 * (shifted(center, 1) - center)
            - (kmid + shifted(kmid, -1)) * 0.5 * (center - shifted(center, -1))
        )
        out_ref[0, i] = center + time_step * (scale * spread - slope)
        return carry

    lax.fori_loop(0, out_ref.shape[1], row, 0, unroll=32)


def stencil_step(conc_pad, start, count, coeff_pad, scale):
    _, px, py, depth = conc_pad.shape
    fields = 4
    assert (coeff_pad.shape[0] - fields) % fields == 0
    coeff_block = (coeff_pad.shape[0] - fields) // fields
    nx, ny = px - 4, py - 4
    return pl.pallas_call(
        stencil_body,
        out_shape=jax.ShapeDtypeStruct((count, nx, ny, depth), jnp.float32),
        grid=(count,),
        in_specs=[
            pl.BlockSpec(memory_space=pltpu.SMEM),
            pl.BlockSpec((1, px, py, depth), lambda s: (s + start, 0, 0, 0)),
            pl.BlockSpec((fields, px, py, depth), lambda s: (coeff_block, 0, 0, 0)),
        ],
        out_specs=pl.BlockSpec((1, nx, ny, depth), lambda s: (s, 0, 0, 0)),
        compiler_params=pltpu.CompilerParams(vmem_limit_bytes=48 * 1024 * 1024),
        cost_estimate=pl.CostEstimate(
            flops=80 * count * nx * ny * depth,
            transcendentals=0,
            bytes_accessed=4 * (2 * count + fields) * px * py * depth,
        ),
    )(scale, conc_pad, coeff_pad)


def basis_body(mix_ref, xt_ref, out_ref):
    for a in range(xt_ref.shape[0]):
        xa = xt_ref[a]
        res = jnp.dot(mix_ref[0], xa, preferred_element_type=jnp.float32)
        res = res + jnp.dot(mix_ref[1], xa, preferred_element_type=jnp.float32)
        res = res + jnp.dot(mix_ref[2], xa, preferred_element_type=jnp.float32)
        out_ref[:, a, :] = res


def basis_rows(mix_ext, static):
    hi = lax.reduce_precision(mix_ext, exponent_bits=8, mantissa_bits=7)
    rem = mix_ext - hi
    mid = lax.reduce_precision(rem, exponent_bits=8, mantissa_bits=7)
    lo = rem - mid
    parts = jnp.stack([hi, mid, lo], 0).astype(jnp.bfloat16)
    xt = jnp.transpose(static, (1, 0, 2))
    span, width, cols = xt.shape
    rows = mix_ext.shape[0]
    block = 8
    return pl.pallas_call(
        basis_body,
        out_shape=jax.ShapeDtypeStruct((rows, span, cols), jnp.float32),
        grid=(span // block,),
        in_specs=[
            pl.BlockSpec(parts.shape, lambda i: (0, 0, 0)),
            pl.BlockSpec((block, width, cols), lambda i: (i, 0, 0)),
        ],
        out_specs=pl.BlockSpec((rows, block, cols), lambda i: (0, i, 0)),
        compiler_params=pltpu.CompilerParams(vmem_limit_bytes=48 * 1024 * 1024),
        cost_estimate=pl.CostEstimate(
            flops=6 * rows * width * span * cols,
            transcendentals=0,
            bytes_accessed=2 * xt.size + 4 * rows * span * cols,
        ),
    )(parts, xt)


def per_device(scalars, velocity, diffusivity, diff_scale, basis_old, sing_values, stored):
    rank = basis_old.shape[0]
    snaps = stored.shape[0]
    static = jnp.concatenate([basis_old, stored], 0)
    weight = jnp.concatenate([sing_values, jnp.ones((snaps,), jnp.float32)], 0)
    total_rows = static.shape[1] * static.shape[2] * lax.axis_size("gx") * lax.axis_size("gy")

    local_gram = lax.dot_general(
        static, static, (((1, 2), (1, 2)), ((), ())), preferred_element_type=jnp.float32
    )
    coeffs = jnp.concatenate([velocity, diffusivity[None]], 0)
    count = scalars.shape[0]
    first = halo(jnp.concatenate([scalars, coeffs], 0))
    middle0 = stencil_step(first, 0, 1, first, diff_scale[:1])
    local_gram, middle0 = lax.optimization_barrier((local_gram, middle0))
    gram_static = butterfly_sum(local_gram) * (weight[:, None] * weight[None, :]) / total_rows
    lower_static = jnp.linalg.cholesky(gram_static)
    width = rank + snaps
    inv_static = lax.linalg.triangular_solve(
        lower_static, jnp.eye(width, dtype=jnp.float32), left_side=True, lower=True
    )
    mix = inv_static * weight[None, :]
    mix_ext = jnp.concatenate([mix, jnp.zeros((1, width), jnp.float32)], 0)
    basis_ext = basis_rows(mix_ext, static)

    result0 = stencil_step(halo(middle0), 0, 1, first, diff_scale[:1])

    coarse = result0[0, ::2]
    span, depth = coarse.shape[1], coarse.shape[2]
    pick_z = (jnp.arange(depth)[:, None] == 2 * jnp.arange(depth // 2)[None, :]).astype(jnp.float32)
    pick_y = (2 * jnp.arange(span // 2)[:, None] == jnp.arange(span)[None, :]).astype(jnp.float32)
    thin = jnp.einsum("ayz,zk->ayk", coarse, pick_z, precision=lax.Precision.HIGHEST)
    fresh = jnp.einsum("jy,ayk->ajk", pick_y, thin, precision=lax.Precision.HIGHEST).reshape(
        coarse.shape[0], -1
    )
    static_f32 = static.astype(jnp.float32)
    cross = jnp.sum(static_f32 * fresh[None], axis=(1, 2))
    self_dot = jnp.sum(fresh * fresh)
    moments = butterfly_sum(jnp.concatenate([cross, self_dot[None]], 0)) / total_rows
    cross_g = moments[:width] * weight
    self_g = moments[width]

    middle_r = stencil_step(first, 1, count - 1, first, diff_scale[1:])
    result_r = stencil_step(halo(middle_r), 0, count - 1, first, diff_scale[1:])
    result = jnp.concatenate([result0, result_r], 0)

    link = lax.linalg.triangular_solve(
        lower_static, cross_g[:, None], left_side=True, lower=True
    )[:, 0]
    corner = jnp.sqrt(self_g - jnp.sum(link * link))
    lower = jnp.zeros((width + 1, width + 1), jnp.float32)
    lower = lower.at[:width, :width].set(lower_static)
    lower = lower.at[width, :width].set(link)
    lower = lower.at[width, width].set(corner)

    along = jnp.sum(mix * link[:, None], axis=0)
    last = (fresh - jnp.sum(static_f32 * along[:, None, None], axis=0)) / corner
    basis_new = put_last_row(basis_ext, last.reshape((1,) + basis_ext.shape[1:]))
    return (result, basis_new, lower.T)


def solution(mesh):
    return jax.shard_map(
        per_device,
        mesh=mesh,
        in_specs=(
            P(None, "gx", "gy", None),
            P(None, "gx", "gy", None),
            P("gx", "gy", None),
            P(),
            P(None, "gx", "gy"),
            P(),
            P(None, "gx", "gy"),
        ),
        out_specs=(P(None, "gx", "gy", None), P(None, "gx", "gy"), P()),
        check_vma=False,
    )
```

```python
import jax
import jax.numpy as jnp
from jax import lax
from jax.sharding import PartitionSpec as P
from jax.experimental import pallas as pl
from jax.experimental.pallas import tpu as pltpu

time_step = 0.25


def ring(axis):
    count = lax.axis_size(axis)
    forward = [(i, (i + 1) % count) for i in range(count)]
    backward = [(target, source) for source, target in forward]
    return forward, backward


def halo(block, width=2):
    fx, bx = ring("gx")
    fy, by = ring("gy")
    nx, ny = block.shape[1], block.shape[2]
    low_x = lax.ppermute(block[:, nx - width :], "gx", fx)
    high_x = lax.ppermute(block[:, :width], "gx", bx)
    low_y = lax.ppermute(block[:, :, ny - width :], "gy", fy)
    high_y = lax.ppermute(block[:, :, :width], "gy", by)
    rows = jnp.concatenate([low_x, block, high_x], axis=1)
    edge = ((0, 0), (width, width), (0, 0), (0, 0))
    return jnp.concatenate([jnp.pad(low_y, edge), rows, jnp.pad(high_y, edge)], axis=2)


def butterfly_sum(value):
    for axis in ("gx", "gy"):
        count = lax.axis_size(axis)
        bit = 1
        while bit < count:
            pairs = [(i, i ^ bit) for i in range(count)]
            value = value + lax.ppermute(value, axis, pairs)
            bit *= 2
    return value


def put_last_row(basis_ext, last):
    def body(_, last_ref, out_ref):
        out_ref[...] = last_ref[...]

    row = basis_ext.shape[0] - 1
    return pl.pallas_call(
        body,
        out_shape=jax.ShapeDtypeStruct(basis_ext.shape, basis_ext.dtype),
        grid=(1,),
        in_specs=[pl.BlockSpec(memory_space=pl.ANY), pl.BlockSpec(last.shape, lambda i: (0, 0, 0))],
        out_specs=pl.BlockSpec(last.shape, lambda i: (row, 0, 0)),
        input_output_aliases={0: 0},
    )(basis_ext, last)


def tendency(concen, coeffs, diff_scale):
    velocity = coeffs[:3]
    kappa = coeffs[3]
    center = concen[:, 2:-2, 2:-2, :]
    flux_first = velocity[0][None] * concen
    slope = (
        8.0 * (flux_first[:, 3:-1, 2:-2] - flux_first[:, 1:-3, 2:-2])
        - (flux_first[:, 4:, 2:-2] - flux_first[:, :-4, 2:-2])
    ) / 12.0
    flux_second = velocity[1][None] * concen
    slope = (
        slope
        + (
            8.0 * (flux_second[:, 2:-2, 3:-1] - flux_second[:, 2:-2, 1:-3])
            - (flux_second[:, 2:-2, 4:] - flux_second[:, 2:-2, :-4])
        )
        / 12.0
    )
    flux_third = jnp.pad(velocity[2][2:-2, 2:-2][None] * center, ((0, 0), (0, 0), (0, 0), (2, 2)))
    slope = (
        slope
        + (
            8.0 * (flux_third[..., 3:-1] - flux_third[..., 1:-3])
            - (flux_third[..., 4:] - flux_third[..., :-4])
        )
        / 12.0
    )
    kappa_mid = kappa[2:-2, 2:-2][None]
    spread = (kappa_mid + kappa[3:-1, 2:-2][None]) * 0.5 * (concen[:, 3:-1, 2:-2] - center) - (
        kappa_mid + kappa[1:-3, 2:-2][None]
    ) * 0.5 * (center - concen[:, 1:-3, 2:-2])
    spread = (
        spread
        + (kappa_mid + kappa[2:-2, 3:-1][None]) * 0.5 * (concen[:, 2:-2, 3:-1] - center)
        - (kappa_mid + kappa[2:-2, 1:-3][None]) * 0.5 * (center - concen[:, 2:-2, 1:-3])
    )
    kappa_pad = jnp.pad(kappa_mid, ((0, 0), (0, 0), (0, 0), (1, 1)))
    center_pad = jnp.pad(center, ((0, 0), (0, 0), (0, 0), (1, 1)))
    spread = (
        spread
        + (kappa_mid + kappa_pad[..., 2:]) * 0.5 * (center_pad[..., 2:] - center)
        - (kappa_mid + kappa_pad[..., :-2]) * 0.5 * (center - center_pad[..., :-2])
    )
    return center + time_step * (diff_scale[:, None, None, None] * spread - slope)


def stencil_body(scale_ref, conc_ref, coeff_ref, out_ref):
    s = pl.program_id(0)
    scale = scale_ref[s]
    rows = out_ref.shape[2]
    depth = out_ref.shape[3]
    lane = lax.broadcasted_iota(jnp.int32, (rows, depth), 1)

    def shifted(value, d):
        rolled = pltpu.roll(value, (-d) % depth, 1)
        keep = (lane + d >= 0) & (lane + d < depth)
        return jnp.where(keep, rolled, 0.0)

    def row(i, carry):
        def c(dx, dy):
            return conc_ref[0, i + 2 + dx, pl.ds(2 + dy, rows), :]

        def k(field, dx, dy):
            return coeff_ref[field, i + 2 + dx, pl.ds(2 + dy, rows), :]

        center = c(0, 0)

        def f1(d):
            return k(0, d, 0) * c(d, 0)

        slope = 8.0 * (f1(1) - f1(-1)) - (f1(2) - f1(-2))

        def f2(d):
            return k(1, 0, d) * c(0, d)

        slope = slope + (8.0 * (f2(1) - f2(-1)) - (f2(2) - f2(-2)))
        f3 = k(2, 0, 0) * center
        slope = slope + (
            8.0 * (shifted(f3, 1) - shifted(f3, -1)) - (shifted(f3, 2) - shifted(f3, -2))
        )
        slope = slope * (1.0 / 12.0)
        kmid = k(3, 0, 0)
        spread = (kmid + k(3, 1, 0)) * 0.5 * (c(1, 0) - center) - (kmid + k(3, -1, 0)) * 0.5 * (
            center - c(-1, 0)
        )
        spread = (
            spread
            + (kmid + k(3, 0, 1)) * 0.5 * (c(0, 1) - center)
            - (kmid + k(3, 0, -1)) * 0.5 * (center - c(0, -1))
        )
        spread = (
            spread
            + (kmid + shifted(kmid, 1)) * 0.5 * (shifted(center, 1) - center)
            - (kmid + shifted(kmid, -1)) * 0.5 * (center - shifted(center, -1))
        )
        out_ref[0, i] = center + time_step * (scale * spread - slope)
        return carry

    lax.fori_loop(0, out_ref.shape[1], row, 0, unroll=32)


def stencil_step(conc_pad, start, count, coeff_pad, scale):
    _, px, py, depth = conc_pad.shape
    fields = 4
    assert (coeff_pad.shape[0] - fields) % fields == 0
    coeff_block = (coeff_pad.shape[0] - fields) // fields
    nx, ny = px - 4, py - 4
    return pl.pallas_call(
        stencil_body,
        out_shape=jax.ShapeDtypeStruct((count, nx, ny, depth), jnp.float32),
        grid=(count,),
        in_specs=[
            pl.BlockSpec(memory_space=pltpu.SMEM),
            pl.BlockSpec((1, px, py, depth), lambda s: (s + start, 0, 0, 0)),
            pl.BlockSpec((fields, px, py, depth), lambda s: (coeff_block, 0, 0, 0)),
        ],
        out_specs=pl.BlockSpec((1, nx, ny, depth), lambda s: (s, 0, 0, 0)),
        compiler_params=pltpu.CompilerParams(vmem_limit_bytes=48 * 1024 * 1024),
        cost_estimate=pl.CostEstimate(
            flops=80 * count * nx * ny * depth,
            transcendentals=0,
            bytes_accessed=4 * (2 * count + fields) * px * py * depth,
        ),
    )(scale, conc_pad, coeff_pad)


def basis_body(mix_ref, xt_ref, out_ref):
    for a in range(xt_ref.shape[0]):
        xa = xt_ref[a]
        res = jnp.dot(mix_ref[0], xa, preferred_element_type=jnp.float32)
        res = res + jnp.dot(mix_ref[1], xa, preferred_element_type=jnp.float32)
        res = res + jnp.dot(mix_ref[2], xa, preferred_element_type=jnp.float32)
        out_ref[:, a, :] = res


def basis_rows(mix_ext, static):
    hi = lax.reduce_precision(mix_ext, exponent_bits=8, mantissa_bits=7)
    rem = mix_ext - hi
    mid = lax.reduce_precision(rem, exponent_bits=8, mantissa_bits=7)
    lo = rem - mid
    parts = jnp.stack([hi, mid, lo], 0).astype(jnp.bfloat16)
    xt = jnp.transpose(static, (1, 0, 2))
    span, width, cols = xt.shape
    rows = mix_ext.shape[0]
    block = 16
    return pl.pallas_call(
        basis_body,
        out_shape=jax.ShapeDtypeStruct((rows, span, cols), jnp.float32),
        grid=(span // block,),
        in_specs=[
            pl.BlockSpec(parts.shape, lambda i: (0, 0, 0)),
            pl.BlockSpec((block, width, cols), lambda i: (i, 0, 0)),
        ],
        out_specs=pl.BlockSpec((rows, block, cols), lambda i: (0, i, 0)),
        compiler_params=pltpu.CompilerParams(vmem_limit_bytes=48 * 1024 * 1024),
        cost_estimate=pl.CostEstimate(
            flops=6 * rows * width * span * cols,
            transcendentals=0,
            bytes_accessed=2 * xt.size + 4 * rows * span * cols,
        ),
    )(parts, xt)


def per_device(scalars, velocity, diffusivity, diff_scale, basis_old, sing_values, stored):
    rank = basis_old.shape[0]
    snaps = stored.shape[0]
    static = jnp.concatenate([basis_old, stored], 0)
    weight = jnp.concatenate([sing_values, jnp.ones((snaps,), jnp.float32)], 0)
    total_rows = static.shape[1] * static.shape[2] * lax.axis_size("gx") * lax.axis_size("gy")

    local_gram = lax.dot_general(
        static, static, (((1, 2), (1, 2)), ((), ())), preferred_element_type=jnp.float32
    )
    coeffs = jnp.concatenate([velocity, diffusivity[None]], 0)
    count = scalars.shape[0]
    first = halo(jnp.concatenate([scalars, coeffs], 0))
    middle0 = stencil_step(first, 0, 1, first, diff_scale[:1])
    local_gram, middle0 = lax.optimization_barrier((local_gram, middle0))
    gram_static = butterfly_sum(local_gram) * (weight[:, None] * weight[None, :]) / total_rows
    lower_static = jnp.linalg.cholesky(gram_static)
    width = rank + snaps
    inv_static = lax.linalg.triangular_solve(
        lower_static, jnp.eye(width, dtype=jnp.float32), left_side=True, lower=True
    )
    mix = inv_static * weight[None, :]
    mix_ext = jnp.concatenate([mix, jnp.zeros((1, width), jnp.float32)], 0)
    basis_ext = basis_rows(mix_ext, static)

    result0 = stencil_step(halo(middle0), 0, 1, first, diff_scale[:1])

    coarse = result0[0, ::2]
    span, depth = coarse.shape[1], coarse.shape[2]
    pick_z = (jnp.arange(depth)[:, None] == 2 * jnp.arange(depth // 2)[None, :]).astype(jnp.float32)
    pick_y = (2 * jnp.arange(span // 2)[:, None] == jnp.arange(span)[None, :]).astype(jnp.float32)
    thin = jnp.einsum("ayz,zk->ayk", coarse, pick_z, precision=lax.Precision.HIGHEST)
    fresh = jnp.einsum("jy,ayk->ajk", pick_y, thin, precision=lax.Precision.HIGHEST).reshape(
        coarse.shape[0], -1
    )
    static_f32 = static.astype(jnp.float32)
    cross = jnp.sum(static_f32 * fresh[None], axis=(1, 2))
    self_dot = jnp.sum(fresh * fresh)
    moments = butterfly_sum(jnp.concatenate([cross, self_dot[None]], 0)) / total_rows
    cross_g = moments[:width] * weight
    self_g = moments[width]

    middle_r = stencil_step(first, 1, count - 1, first, diff_scale[1:])
    result_r = stencil_step(halo(middle_r), 0, count - 1, first, diff_scale[1:])
    result = jnp.concatenate([result0, result_r], 0)

    link = lax.linalg.triangular_solve(
        lower_static, cross_g[:, None], left_side=True, lower=True
    )[:, 0]
    corner = jnp.sqrt(self_g - jnp.sum(link * link))
    lower = jnp.zeros((width + 1, width + 1), jnp.float32)
    lower = lower.at[:width, :width].set(lower_static)
    lower = lower.at[width, :width].set(link)
    lower = lower.at[width, width].set(corner)

    along = jnp.sum(mix * link[:, None], axis=0)
    last = (fresh - jnp.sum(static_f32 * along[:, None, None], axis=0)) / corner
    basis_new = put_last_row(basis_ext, last.reshape((1,) + basis_ext.shape[1:]))
    return (result, basis_new, lower.T)


def solution(mesh):
    return jax.shard_map(
        per_device,
        mesh=mesh,
        in_specs=(
            P(None, "gx", "gy", None),
            P(None, "gx", "gy", None),
            P("gx", "gy", None),
            P(),
            P(None, "gx", "gy"),
            P(),
            P(None, "gx", "gy"),
        ),
        out_specs=(P(None, "gx", "gy", None), P(None, "gx", "gy"), P()),
        check_vma=False,
    )
```
